128 devices in a mesh: ctx: 32 (over x, y, core), head: 4 (over z).
Axes of the slice: x: 4, y: 4, z: 4, core: 2. Of those that a mesh axis runs over, the one named last changes fastest.
Arguments:
- x_in: bfloat16 [16384, 1, 8192], P('ctx', None, 'head'), may hold values from -6 to 6
- z_in: bfloat16 [16384, 1, 8192], P('ctx', None, 'head')
- bc_in: bfloat16 [16384, 1, 256], P('ctx'), may hold values from -6 to 6
- dt_in: float32 [16384, 1, 128], P('ctx', None, 'head'), may hold values from -3 to 3
- dt_bias: float32 [128], P('head')
- a_log: float32 [128], P('head'), may hold values from -1.5 to 0.5
- skip: float32 [128], P('head'), may hold values from 0.5 to 1.5
- conv_x: bfloat16 [4, 8192], P(None, 'head'), may hold values from -3 to 3
- conv_bc: bfloat16 [4, 256], replicated, may hold values from -3 to 3
- norm_gain: float32 [8192], P('head'), may hold values from 0.1 to 1.9
- w_out: bfloat16 [8192, 4096], P('head'), may hold values from -0.0625 to 0.0625
- requests: int32 [256], P('ctx'), may hold values from 0 to 1, as said below
- step_x: bfloat16 [4, 256, 8192], P(None, 'ctx', 'head'), may hold values from -6 to 6
- step_z: bfloat16 [4, 256, 8192], P(None, 'ctx', 'head'), may hold values from -6 to 6
- step_bc: bfloat16 [4, 256, 256], P(None, 'ctx'), may hold values from -6 to 6
- step_dt: float32 [4, 256, 128], P(None, 'ctx', 'head'), may hold values from -3 to 3
Outputs:
- out: bfloat16 [16384, 1, 4096], P(('ctx', 'head'))
- dec_out: bfloat16 [4, 256, 8192], P(None, 'ctx', 'head')
The draws below stay inside these ranges and needn't reach their ends.
Inputs may be any that keep to these rules, and one draw needn't show every extreme that they name: Slot r is decoded on index r // 8 of ctx. Each index's 8 slots hold its requests first, then empty slots marked 1; every index has one request or more, and some index has all 8 slots in use.
All inputs are finite; a program needn't handle non-finite values.
Results may differ from the reference program's by a relative error of at most 0.007.
Values may be sent and summed in bfloat16 or wider, within the bound.
No kernel may reach another device: no remote copies, remote signals or barrier semaphores. Data moves between devices by JAX's collectives and lax.ppermute only.
A program may use at most 256 MiB of HBM per device.

```python
import jax
import jax.numpy as jnp
from jax import lax

D = 4096
HEADS = 128
HEAD_DIM = 64
STATE = 128
CONV = 4
BLOCK = 512
PROMPTS = 1
SLOTS = 8
STEPS = 4
INNER = 8192
LEN = 16384
NREQ = 256


latent_terms = 16


latent_share = 0.866


noise_share = 0.5


def latent_parts(key):
    key_sign, key_x, key_b = jax.random.split(jax.random.fold_in(key, 23), 3)
    signs = jnp.where(jax.random.bernoulli(key_sign, 0.5, (LEN, PROMPTS, latent_terms)), 1.0, -1.0).astype(jnp.float32)
    table_x = jax.random.normal(key_x, (latent_terms, INNER), jnp.float32) * 0.25
    table_b = jax.random.normal(key_b, (latent_terms, STATE), jnp.float32) * 0.25
    return (signs, table_x, table_b)


def latent_mix(signs, table):
    total = jnp.zeros(signs.shape[:-1] + (table.shape[1],), jnp.float32)
    for term in range(latent_terms):
        total = total + signs[..., term:term + 1] * table[term]
    return total


def unit_noise(key, shape):
    return jax.random.normal(key, shape, jnp.float32)


def draw_x_in(key, part):
    signs, table_x, table_b = latent_parts(key)
    noise = unit_noise(jax.random.fold_in(key, 29), (LEN, PROMPTS, INNER))
    values = latent_share * latent_mix(signs, table_x) + noise_share * noise
    return jnp.clip(values, -6.0, 6.0).astype(jnp.bfloat16)


def draw_bc_in(key, part):
    signs, table_x, table_b = latent_parts(key)
    noise_b = unit_noise(jax.random.fold_in(key, 31), (LEN, PROMPTS, STATE))
    noise_c = unit_noise(jax.random.fold_in(key, 37), (LEN, PROMPTS, STATE))
    b_half = latent_share * latent_mix(signs, table_b) + noise_share * noise_b
    values = jnp.concatenate([b_half, noise_c], axis=-1)
    return jnp.clip(values, -6.0, 6.0).astype(jnp.bfloat16)


def draw_z_in(key, part):
    position = jnp.arange(INNER, dtype=jnp.float32) / INNER
    base_vals = jax.random.normal(key, (LEN, PROMPTS, INNER), jnp.float32)
    scales = jnp.exp(0.7 * position)
    return (base_vals * scales).astype(jnp.bfloat16)


def draw_dt_bias(key, part):
    key_pick, key_fast, key_slow = jax.random.split(jax.random.fold_in(key, 11), 3)
    share = 0.5
    picked = jax.random.bernoulli(key_pick, share, (HEADS,))
    fast_dt = jnp.exp(jax.random.uniform(key_fast, (HEADS,), jnp.float32, jnp.log(0.02), jnp.log(0.2)))
    slow_dt = jnp.exp(jax.random.uniform(key_slow, (HEADS,), jnp.float32, jnp.log(0.3 / LEN), jnp.log(1.2 / LEN)))
    target = jnp.where(picked, fast_dt, slow_dt)
    return jnp.log(jnp.expm1(target)).astype(jnp.float32)


def draw_requests(key, part):
    key_count, key_full, key_ids = jax.random.split(jax.random.fold_in(key, 7), 3)
    devices = NREQ // SLOTS
    counts = jax.random.randint(key_count, (devices,), 1, SLOTS + 1)
    full_index = jax.random.randint(key_full, (), 0, devices)
    counts = jnp.where(jnp.arange(devices) == full_index, SLOTS, counts)
    prompt_ids = jax.random.randint(key_ids, (devices, SLOTS), 0, PROMPTS)
    prompt_ids = jnp.where(jnp.arange(SLOTS)[None, :] < counts[:, None], prompt_ids, PROMPTS)
    return prompt_ids.reshape(NREQ).astype(jnp.int32)


def block_scale(key, extent, cuts, smallest, largest):
    gain = 1.0
    for axis_at, blocks in cuts:
        draws = jax.random.uniform(jax.random.fold_in(jax.random.fold_in(key, 6), axis_at), (blocks,), jnp.float32, smallest / len(cuts), largest / len(cuts))
        gain = gain * jnp.repeat(jnp.exp(draws), extent[axis_at] // blocks).reshape((-1,) + (1,) * (len(extent) - 1 - axis_at))
    return gain


def bell_draw(own_key, dims, scale, reach, cuts=(), held_as=jnp.bfloat16):
    gain = block_scale(own_key, dims, cuts, -0.22, 0.18) if cuts else 1.0
    array = jax.random.normal(own_key, dims, jnp.float32) * scale * gain
    return jnp.minimum(jnp.maximum(array, -reach), reach).astype(held_as)


def setup_inputs(seed: int = 0) -> dict:
    seeds = jax.random.split(jax.random.key(seed), 17)
    x_in = draw_x_in(jax.random.fold_in(seeds[16], 71), 0)
    z_in = draw_z_in(jax.random.fold_in(seeds[16], 71), 0)
    bc_in = draw_bc_in(jax.random.fold_in(seeds[16], 71), 0)
    dt_in = bell_draw(seeds[3], (LEN, PROMPTS, HEADS), 0.7, 3.0, ((0, 32), (2, 4)), jnp.float32)
    dt_bias = draw_dt_bias(jax.random.fold_in(seeds[16], 71), 0)
    a_log = jnp.clip(-1.5 + 2.0 * jax.random.uniform(seeds[5], (HEADS,), jnp.float32) ** block_scale(seeds[5], (HEADS,), ((0, 4),), -0.2, 0.2), -1.5, 0.5)
    skip = jnp.clip(0.5 + 1.0 * jax.random.uniform(seeds[6], (HEADS,), jnp.float32) ** block_scale(seeds[6], (HEADS,), ((0, 4),), -0.2, 0.2), 0.5, 1.5)
    conv_x = bell_draw(seeds[7], (CONV, INNER), CONV ** -0.5, 3.0, ((1, 4),))
    conv_bc = bell_draw(seeds[8], (CONV, 2 * STATE), CONV ** -0.5, 3.0)
    norm_gain = jnp.clip(1.0 + 0.18 * jax.random.normal(seeds[9], (INNER,), jnp.float32), 0.1, 1.9)
    w_out = bell_draw(seeds[10], (INNER, D), INNER ** -0.5, 0.0625, ((0, 4),))
    requests = draw_requests(jax.random.fold_in(seeds[16], 71), 0)
    step_x = bell_draw(seeds[12], (STEPS, NREQ, INNER), 1.0, 6.0, ((1, 32), (2, 4)))
    step_z = bell_draw(seeds[13], (STEPS, NREQ, INNER), 1.0, 6.0, ((1, 32), (2, 4)))
    step_bc = bell_draw(seeds[14], (STEPS, NREQ, 2 * STATE), 1.0, 6.0, ((1, 32),))
    step_dt = bell_draw(seeds[15], (STEPS, NREQ, HEADS), 0.7, 3.0, ((1, 32), (2, 4)), jnp.float32)
    return {"x_in": x_in, "z_in": z_in, "bc_in": bc_in, "dt_in": dt_in, "dt_bias": dt_bias, "a_log": a_log, "skip": skip, "conv_x": conv_x, "conv_bc": conv_bc, "norm_gain": norm_gain, "w_out": w_out, "requests": requests, "step_x": step_x, "step_z": step_z, "step_bc": step_bc, "step_dt": step_dt}


def conv_silu(window, weight, length):
    running_sum = jnp.zeros((length,) + window.shape[1:], jnp.float32)
    for offset in range(weight.shape[0]):
        running_sum = running_sum + window[offset:offset + length].astype(jnp.float32) * weight[offset].astype(jnp.float32)
    return jax.nn.silu(running_sum).astype(jnp.bfloat16)

def reference(x_in, z_in, bc_in, dt_in, dt_bias, a_log, skip, conv_x, conv_bc, norm_gain, w_out, requests, step_x, step_z, step_bc, step_dt):
    x_conv = conv_silu(jnp.concatenate([jnp.zeros((CONV - 1, PROMPTS, INNER), jnp.bfloat16), x_in], axis=0), conv_x, LEN)
    bc_conv = conv_silu(jnp.concatenate([jnp.zeros((CONV - 1, PROMPTS, 2 * STATE), jnp.bfloat16), bc_in], axis=0), conv_bc, LEN)
    decay_rates = -jnp.exp(a_log)
    dt_full = jax.nn.softplus(dt_in + dt_bias)
    num_blocks = LEN // BLOCK
    pieces_all = (x_conv.reshape(num_blocks, BLOCK, PROMPTS, INNER), bc_conv.reshape(num_blocks, BLOCK, PROMPTS, 2 * STATE), dt_full.reshape(num_blocks, BLOCK, PROMPTS, HEADS), z_in.reshape(num_blocks, BLOCK, PROMPTS, INNER))
    position = lax.iota(jnp.int32, BLOCK)
    causal = position[:, None] >= position[None, :]

    def one_block(state_now, pieces):
        x_blk, bc_blk, dt_blk, z_blk = pieces
        b_rows = bc_blk[..., :STATE]
        c_rows = bc_blk[..., STATE:]
        cum_log = jnp.cumsum(dt_blk * decay_rates, axis=0)
        cum_heads = jnp.transpose(cum_log, (1, 2, 0))
        dt_heads = jnp.transpose(dt_blk, (1, 2, 0))
        x_heads = x_blk.reshape(BLOCK, PROMPTS, HEADS, HEAD_DIM)
        scores = jnp.einsum('ipn,jpn->pij', c_rows.astype(jnp.float32), b_rows.astype(jnp.float32))
        gaps = jnp.where(causal, cum_heads[..., :, None] - cum_heads[..., None, :], -jnp.inf)
        mixing = (scores[:, None] * jnp.exp(gaps) * dt_heads[..., None, :]).astype(jnp.bfloat16)
        y_intra = jnp.einsum('phij,jphd->iphd', mixing.astype(jnp.float32), x_heads.astype(jnp.float32))
        block_log = cum_heads[..., -1]
        tail_weights = jnp.transpose(jnp.exp(block_log[..., None] - cum_heads) * dt_heads, (2, 0, 1))
        weighted_x = (x_heads.astype(jnp.float32) * tail_weights[..., None]).astype(jnp.bfloat16)
        s_local = jnp.einsum('jphd,jpn->phdn', weighted_x.astype(jnp.float32), b_rows.astype(jnp.float32))
        y_inter = jnp.einsum('ipn,phdn->iphd', c_rows.astype(jnp.float32), state_now, precision=lax.Precision.HIGHEST) * jnp.exp(cum_log)[..., None]
        y_all = y_intra + y_inter + skip[:, None] * x_heads.astype(jnp.float32)
        gated_out = y_all.reshape(BLOCK, PROMPTS, INNER) * jax.nn.silu(z_blk.astype(jnp.float32))
        mean_square = lax.optimization_barrier(jnp.mean(gated_out * gated_out, axis=-1))
        normed = (gated_out * lax.rsqrt(mean_square + 1e-05)[..., None] * norm_gain).astype(jnp.bfloat16)
        out_blk = jnp.dot(normed.reshape(BLOCK * PROMPTS, INNER), w_out, preferred_element_type=jnp.float32)
        out_blk = out_blk.reshape(BLOCK, PROMPTS, D).astype(jnp.bfloat16)
        state_next = jnp.exp(block_log)[..., None, None] * state_now + s_local
        return (state_next, out_blk)
    final_state, out_blocks = lax.scan(one_block, jnp.zeros((PROMPTS, HEADS, HEAD_DIM, STATE), jnp.float32), pieces_all)
    out = out_blocks.reshape(LEN, PROMPTS, D)
    final_x = x_in[LEN - CONV + 1:].astype(jnp.float32)
    final_bc = bc_in[LEN - CONV + 1:].astype(jnp.float32)
    slot_pick = (requests[:, None] == lax.iota(jnp.int32, PROMPTS)[None, :]).astype(jnp.float32)
    live_slots = requests < PROMPTS
    states = jnp.einsum('rp,phdn->rhdn', slot_pick, final_state, precision=lax.Precision.HIGHEST)
    hist_x = jnp.einsum('rp,kpi->kri', slot_pick, final_x, precision=lax.Precision.HIGHEST).astype(jnp.bfloat16)
    hist_bc = jnp.einsum('rp,kpi->kri', slot_pick, final_bc, precision=lax.Precision.HIGHEST).astype(jnp.bfloat16)
    outputs = []
    for step_index in range(STEPS):
        window_x = jnp.concatenate([hist_x, step_x[step_index][None]], axis=0)
        window_bc = jnp.concatenate([hist_bc, step_bc[step_index][None]], axis=0)
        new_x = conv_silu(window_x, conv_x, 1)[0]
        new_bc = conv_silu(window_bc, conv_bc, 1)[0]
        hist_x = window_x[1:]
        hist_bc = window_bc[1:]
        dt_step = jax.nn.softplus(step_dt[step_index] + dt_bias)
        x_step = new_x.reshape(NREQ, HEADS, HEAD_DIM).astype(jnp.float32)
        b_step = new_bc[:, :STATE].astype(jnp.float32)
        c_step = new_bc[:, STATE:].astype(jnp.float32)
        states = jnp.exp(dt_step * decay_rates)[..., None, None] * states + (dt_step[..., None] * x_step)[..., None] * b_step[:, None, None, :]
        y_step = jnp.einsum('rn,rhdn->rhd', c_step, states, precision=lax.Precision.HIGHEST) + skip[:, None] * x_step
        gated_step = y_step.reshape(NREQ, INNER) * jax.nn.silu(step_z[step_index].astype(jnp.float32))
        outputs.append(jnp.where(live_slots[:, None], gated_step, 0.0).astype(jnp.bfloat16))
    return (out, jnp.stack(outputs))
```

```python
import jax
import jax.numpy as jnp
from jax import lax
from jax.sharding import PartitionSpec as P

norm_eps = 1e-05


def passed_along(value, axis, steps):
    count = lax.axis_size(axis)
    leading, last = (max(0, -steps), min(count, count - steps))
    return lax.ppermute(value, axis, [(source, source + steps) for source in range(leading, last)])


def group_shift(value, axis, count, stride, group, shift):
    pairs = []
    for source in range(count):
        member = (source // stride) % group
        target = source + (((member + shift) % group) - member) * stride
        pairs.append((source, target))
    return lax.ppermute(value, axis, pairs)


def conv_silu(window, weight, length):
    running_sum = jnp.zeros((length,) + window.shape[1:], jnp.float32)
    for offset in range(weight.shape[0]):
        running_sum = running_sum + window[offset : offset + length].astype(jnp.float32) * weight[
            offset
        ].astype(jnp.float32)
    return jax.nn.silu(running_sum).astype(jnp.bfloat16)


def chain(earlier, later):
    return (earlier[0] * later[0], later[0][..., None, None] * earlier[1] + later[1])


def pick(flag, first, second):
    return jax.tree.map(lambda a, b: jnp.where(flag, a, b), first, second)


def ring_scan(own, tails, axis, count, stride, group):
    member = (lax.axis_index(axis) // stride) % group
    received = [None] + [
        group_shift((own, tails), axis, count, stride, group, shift) for shift in range(1, group)
    ]
    identity = (jnp.ones_like(own[0]), jnp.zeros_like(own[1]))
    before = identity
    for shift in range(group - 1, 0, -1):
        before = pick(shift <= member, chain(before, received[shift][0]), before)
    total = chain(before, own)
    for shift in range(group - 1, 0, -1):
        total = pick(shift > member, chain(total, received[shift][0]), total)
    last_tails = tails
    for shift in range(1, group):
        last_tails = pick((member - shift) % group == group - 1, received[shift][1], last_tails)
    return before, total, last_tails


def body(
    x_in,
    z_in,
    bc_in,
    dt_in,
    dt_bias,
    a_log,
    skip,
    conv_x,
    conv_bc,
    norm_gain,
    w_out,
    requests,
    step_x,
    step_z,
    step_bc,
    step_dt,
):
    block_len, prompts, inner_loc = x_in.shape
    heads_loc = dt_in.shape[2]
    head_dim = inner_loc // heads_loc
    state_dim = bc_in.shape[2] // 2
    conv_taps = conv_x.shape[0]
    edge_x, edge_bc = passed_along(
        (x_in[block_len - conv_taps + 1 :], bc_in[block_len - conv_taps + 1 :]), "ctx", 1
    )
    x_conv = conv_silu(jnp.concatenate([edge_x, x_in], axis=0), conv_x, block_len)
    bc_conv = conv_silu(jnp.concatenate([edge_bc, bc_in], axis=0), conv_bc, block_len)
    b_rows = bc_conv[..., :state_dim]
    c_rows = bc_conv[..., state_dim:]
    decay_rates = -jnp.exp(a_log)
    dt_full = jax.nn.softplus(dt_in + dt_bias)
    cum_log = jnp.cumsum(dt_full * decay_rates, axis=0)
    cum_heads = jnp.transpose(cum_log, (1, 2, 0))
    dt_heads = jnp.transpose(dt_full, (1, 2, 0))
    x_heads = x_conv.reshape(block_len, prompts, heads_loc, head_dim)
    block_log = cum_heads[..., -1]
    tail_weights = jnp.transpose(jnp.exp(block_log[..., None] - cum_heads) * dt_heads, (2, 0, 1))
    weighted_x = (x_heads * tail_weights[..., None]).astype(jnp.bfloat16)
    s_local = jnp.einsum("jphd,jpn->phdn", weighted_x, b_rows, preferred_element_type=jnp.float32)
    block_decay = jnp.exp(block_log)

    count = lax.axis_size("ctx")
    here = lax.axis_index("ctx")
    core = here % 2
    tails = (x_in[block_len - conv_taps + 1 :], bc_in[block_len - conv_taps + 1 :])
    own = (block_decay, s_local)
    other, other_tails = group_shift((own, tails), "ctx", count, 1, 2, 1)
    first = pick(core == 0, own, other)
    second = pick(core == 0, other, own)
    chip_total = chain(first, second)
    chip_tails = pick(core == 0, other_tails, tails)
    half = state_dim // 2
    chip_half = (
        chip_total[0],
        jnp.where(core == 0, chip_total[1][..., :half], chip_total[1][..., half:]),
    )
    row_before, row_total, row_tails = ring_scan(chip_half, chip_tails, "ctx", count, 2, 4)
    rows = count // 8
    top_before, top_total, final_tails = ring_scan(row_total, row_tails, "ctx", count, 8, rows)
    chip_before = chain(top_before, row_before)
    mine = (chip_before[1], top_total[1])
    theirs = group_shift(mine, "ctx", count, 1, 2, 1)
    joined = jax.tree.map(
        lambda a, b: jnp.where(core == 0, jnp.concatenate([a, b], -1), jnp.concatenate([b, a], -1)),
        mine,
        theirs,
    )
    chip_state, final_state = joined
    s_before = jnp.where(
        core == 0, chip_state, first[0][..., None, None] * chip_state + first[1]
    )

    scores = jnp.einsum("ipn,jpn->pij", c_rows, b_rows, preferred_element_type=jnp.float32)
    position = lax.iota(jnp.int32, block_len)
    causal = position[:, None] >= position[None, :]
    gaps = jnp.where(causal, cum_heads[..., :, None] - cum_heads[..., None, :], -jnp.inf)
    mixing = (scores[:, None] * jnp.exp(gaps) * dt_heads[..., None, :]).astype(jnp.bfloat16)
    y_intra = jnp.einsum("phij,jphd->iphd", mixing, x_heads, preferred_element_type=jnp.float32)
    y_inter = (
        jnp.einsum(
            "ipn,phdn->iphd", c_rows.astype(jnp.float32), s_before, precision=lax.Precision.HIGHEST
        )
        * jnp.exp(cum_log)[..., None]
    )
    y_all = y_intra + y_inter + skip[:, None] * x_heads.astype(jnp.float32)
    gated_out = y_all.reshape(block_len, prompts, inner_loc) * jax.nn.silu(z_in.astype(jnp.float32))
    square_sums = lax.psum(jnp.sum(gated_out * gated_out, axis=-1), "head")
    inner_total = inner_loc * lax.axis_size("head")
    normed = (
        gated_out * lax.rsqrt(square_sums / inner_total + norm_eps)[..., None] * norm_gain
    ).astype(jnp.bfloat16)
    projected = lax.psum_scatter(
        jnp.einsum("tpi,id->tpd", normed, w_out, preferred_element_type=jnp.float32),
        "head",
        scatter_dimension=0,
        tiled=True,
    )
    out = projected.astype(jnp.bfloat16)

    final_x, final_bc = final_tails
    slot_count = requests.shape[0]
    steps = step_x.shape[0]
    slot_pick = (requests[:, None] == lax.iota(jnp.int32, prompts)[None, :]).astype(jnp.float32)
    live_slots = requests < prompts
    hist_x = jnp.einsum(
        "rp,kpi->kri", slot_pick, final_x.astype(jnp.float32), precision=lax.Precision.HIGHEST
    ).astype(jnp.bfloat16)
    hist_bc = jnp.einsum(
        "rp,kpi->kri", slot_pick, final_bc.astype(jnp.float32), precision=lax.Precision.HIGHEST
    ).astype(jnp.bfloat16)
    window_x = jnp.concatenate([hist_x, step_x], axis=0)
    window_bc = jnp.concatenate([hist_bc, step_bc], axis=0)
    new_x = conv_silu(window_x, conv_x, steps)
    new_bc = conv_silu(window_bc, conv_bc, steps)
    dt_step = jax.nn.softplus(step_dt + dt_bias)
    x_step = new_x.reshape(steps, slot_count, heads_loc, head_dim).astype(jnp.float32)
    b_step = new_bc[..., :state_dim].astype(jnp.float32)
    c_step = new_bc[..., state_dim:].astype(jnp.float32)
    step_decay = jnp.exp(dt_step * decay_rates)
    pushed = dt_step[..., None] * x_step
    from_final = jnp.einsum(
        "phdn,srn->psrhd", final_state.reshape(prompts, heads_loc, head_dim, state_dim), c_step,
        precision=lax.Precision.HIGHEST,
    )
    from_final = jnp.einsum("rp,psrhd->srhd", slot_pick, from_final, precision=lax.Precision.HIGHEST)
    overlap = jnp.einsum("trn,srn->tsr", b_step, c_step, precision=lax.Precision.HIGHEST)
    outputs = []
    carried = jnp.ones_like(step_decay[0])
    for step_index in range(steps):
        carried = carried * step_decay[step_index]
        y_step = carried[..., None] * from_final[step_index]
        for earlier in range(step_index + 1):
            weight = jnp.ones_like(step_decay[0])
            for later in range(earlier + 1, step_index + 1):
                weight = weight * step_decay[later]
            y_step = y_step + (weight * overlap[earlier, step_index][:, None])[..., None] * pushed[
                earlier
            ]
        y_step = y_step + skip[:, None] * x_step[step_index]
        gated_step = y_step.reshape(slot_count, inner_loc) * jax.nn.silu(
            step_z[step_index].astype(jnp.float32)
        )
        outputs.append(jnp.where(live_slots[:, None], gated_step, 0.0).astype(jnp.bfloat16))
    return (out, jnp.stack(outputs))

def solution(mesh):
    placed = (
        P("ctx", None, "head"),
        P("ctx", None, "head"),
        P("ctx", None, None),
        P("ctx", None, "head"),
        P("head"),
        P("head"),
        P("head"),
        P(None, "head"),
        P(),
        P("head"),
        P("head", None),
        P("ctx"),
        P(None, "ctx", "head"),
        P(None, "ctx", "head"),
        P(None, "ctx", None),
        P(None, "ctx", "head"),
    )
    return jax.shard_map(
        body,
        mesh=mesh,
        in_specs=placed,
        out_specs=(P(("ctx", "head"), None, None), P(None, "ctx", "head")),
        check_vma=False,
    )
```

```python
import jax
import jax.numpy as jnp
from jax import lax
from jax.sharding import PartitionSpec as P

norm_eps = 1e-05


def passed_along(value, axis, steps):
    count = lax.axis_size(axis)
    leading, last = (max(0, -steps), min(count, count - steps))
    return lax.ppermute(value, axis, [(source, source + steps) for source in range(leading, last)])


def group_shift(value, axis, count, stride, group, shift):
    pairs = []
    for source in range(count):
        member = (source // stride) % group
        target = source + (((member + shift) % group) - member) * stride
        pairs.append((source, target))
    return lax.ppermute(value, axis, pairs)


def conv_silu(window, weight, length):
    running_sum = jnp.zeros((length,) + window.shape[1:], jnp.float32)
    for offset in range(weight.shape[0]):
        running_sum = running_sum + window[offset : offset + length].astype(jnp.float32) * weight[
            offset
        ].astype(jnp.float32)
    return jax.nn.silu(running_sum).astype(jnp.bfloat16)


def chain(earlier, later):
    return (earlier[0] * later[0], later[0][..., None, None] * earlier[1] + later[1])


def pick(flag, first, second):
    return jax.tree.map(lambda a, b: jnp.where(flag, a, b), first, second)


def ring_scan(own, tails, axis, count, stride, group):
    member = (lax.axis_index(axis) // stride) % group
    message = (own, tails)
    if group == 4:
        from_prev = group_shift(message, axis, count, stride, group, 1)
        from_next = group_shift(message, axis, count, stride, group, -1)
        split = own[1].shape[-1] // 2
        lead = group_shift(
            (from_prev[0][0], from_prev[0][1][..., :split], from_prev[1]),
            axis, count, stride, group, 1,
        )
        rest = group_shift(from_next[0][1][..., split:], axis, count, stride, group, -1)
        far = ((lead[0], jnp.concatenate([lead[1], rest], -1)), lead[2])
        received = [None, from_prev, far, from_next]
    else:
        received = [None] + [
            group_shift(message, axis, count, stride, group, shift) for shift in range(1, group)
        ]
    identity = (jnp.ones_like(own[0]), jnp.zeros_like(own[1]))
    before = identity
    for shift in range(group - 1, 0, -1):
        before = pick(shift <= member, chain(before, received[shift][0]), before)
    total = chain(before, own)
    for shift in range(group - 1, 0, -1):
        total = pick(shift > member, chain(total, received[shift][0]), total)
    last_tails = tails
    for shift in range(1, group):
        last_tails = pick((member - shift) % group == group - 1, received[shift][1], last_tails)
    return before, total, last_tails


def body(
    x_in,
    z_in,
    bc_in,
    dt_in,
    dt_bias,
    a_log,
    skip,
    conv_x,
    conv_bc,
    norm_gain,
    w_out,
    requests,
    step_x,
    step_z,
    step_bc,
    step_dt,
):
    block_len, prompts, inner_loc = x_in.shape
    heads_loc = dt_in.shape[2]
    head_dim = inner_loc // heads_loc
    state_dim = bc_in.shape[2] // 2
    conv_taps = conv_x.shape[0]
    edge_x, edge_bc = passed_along(
        (x_in[block_len - conv_taps + 1 :], bc_in[block_len - conv_taps + 1 :]), "ctx", 1
    )
    x_conv = conv_silu(jnp.concatenate([edge_x, x_in], axis=0), conv_x, block_len)
    bc_conv = conv_silu(jnp.concatenate([edge_bc, bc_in], axis=0), conv_bc, block_len)
    b_rows = bc_conv[..., :state_dim]
    c_rows = bc_conv[..., state_dim:]
    decay_rates = -jnp.exp(a_log)
    dt_full = jax.nn.softplus(dt_in + dt_bias)
    cum_log = jnp.cumsum(dt_full * decay_rates, axis=0)
    cum_heads = jnp.transpose(cum_log, (1, 2, 0))
    dt_heads = jnp.transpose(dt_full, (1, 2, 0))
    x_heads = x_conv.reshape(block_len, prompts, heads_loc, head_dim)
    block_log = cum_heads[..., -1]
    tail_weights = jnp.transpose(jnp.exp(block_log[..., None] - cum_heads) * dt_heads, (2, 0, 1))
    weighted_x = (x_heads * tail_weights[..., None]).astype(jnp.bfloat16)
    s_local = jnp.einsum("jphd,jpn->phdn", weighted_x, b_rows, preferred_element_type=jnp.float32)
    block_decay = jnp.exp(block_log)

    count = lax.axis_size("ctx")
    here = lax.axis_index("ctx")
    core = here % 2
    tails = (x_in[block_len - conv_taps + 1 :], bc_in[block_len - conv_taps + 1 :])
    own = (block_decay, s_local)
    other, other_tails = group_shift((own, tails), "ctx", count, 1, 2, 1)
    first = pick(core == 0, own, other)
    second = pick(core == 0, other, own)
    chip_total = chain(first, second)
    chip_tails = pick(core == 0, other_tails, tails)
    half = state_dim // 2
    chip_half = (
        chip_total[0],
        jnp.where(core == 0, chip_total[1][..., :half], chip_total[1][..., half:]),
    )
    row_before, row_total, row_tails = ring_scan(chip_half, chip_tails, "ctx", count, 2, 4)
    rows = count // 8
    top_before, top_total, final_tails = ring_scan(row_total, row_tails, "ctx", count, 8, rows)
    chip_before = chain(top_before, row_before)
    mine = (chip_before[1], top_total[1])
    theirs = group_shift(mine, "ctx", count, 1, 2, 1)
    joined = jax.tree.map(
        lambda a, b: jnp.where(core == 0, jnp.concatenate([a, b], -1), jnp.concatenate([b, a], -1)),
        mine,
        theirs,
    )
    chip_state, final_state = joined
    s_before = jnp.where(
        core == 0, chip_state, first[0][..., None, None] * chip_state + first[1]
    )

    scores = jnp.einsum("ipn,jpn->pij", c_rows, b_rows, preferred_element_type=jnp.float32)
    position = lax.iota(jnp.int32, block_len)
    causal = position[:, None] >= position[None, :]
    gaps = jnp.where(causal, cum_heads[..., :, None] - cum_heads[..., None, :], -jnp.inf)
    mixing = (scores[:, None] * jnp.exp(gaps) * dt_heads[..., None, :]).astype(jnp.bfloat16)
    y_intra = jnp.einsum("phij,jphd->iphd", mixing, x_heads, preferred_element_type=jnp.float32)
    y_inter = (
        jnp.einsum(
            "ipn,phdn->iphd", c_rows.astype(jnp.float32), s_before, precision=lax.Precision.HIGHEST
        )
        * jnp.exp(cum_log)[..., None]
    )
    y_all = y_intra + y_inter + skip[:, None] * x_heads.astype(jnp.float32)
    gated_out = y_all.reshape(block_len, prompts, inner_loc) * jax.nn.silu(z_in.astype(jnp.float32))
    square_sums = lax.psum(jnp.sum(gated_out * gated_out, axis=-1), "head")
    inner_total = inner_loc * lax.axis_size("head")
    normed = (
        gated_out * lax.rsqrt(square_sums / inner_total + norm_eps)[..., None] * norm_gain
    ).astype(jnp.bfloat16)
    projected = lax.psum_scatter(
        jnp.einsum("tpi,id->tpd", normed, w_out, preferred_element_type=jnp.float32).astype(
            jnp.bfloat16
        ),
        "head",
        scatter_dimension=0,
        tiled=True,
    )
    out = projected.astype(jnp.bfloat16)

    final_x, final_bc = final_tails
    slot_count = requests.shape[0]
    steps = step_x.shape[0]
    slot_pick = (requests[:, None] == lax.iota(jnp.int32, prompts)[None, :]).astype(jnp.float32)
    live_slots = requests < prompts
    hist_x = jnp.einsum(
        "rp,kpi->kri", slot_pick, final_x.astype(jnp.float32), precision=lax.Precision.HIGHEST
    ).astype(jnp.bfloat16)
    hist_bc = jnp.einsum(
        "rp,kpi->kri", slot_pick, final_bc.astype(jnp.float32), precision=lax.Precision.HIGHEST
    ).astype(jnp.bfloat16)
    window_x = jnp.concatenate([hist_x, step_x], axis=0)
    window_bc = jnp.concatenate([hist_bc, step_bc], axis=0)
    new_x = conv_silu(window_x, conv_x, steps)
    new_bc = conv_silu(window_bc, conv_bc, steps)
    dt_step = jax.nn.softplus(step_dt + dt_bias)
    x_step = new_x.reshape(steps, slot_count, heads_loc, head_dim).astype(jnp.float32)
    b_step = new_bc[..., :state_dim].astype(jnp.float32)
    c_step = new_bc[..., state_dim:].astype(jnp.float32)
    step_decay = jnp.exp(dt_step * decay_rates)
    pushed = dt_step[..., None] * x_step
    from_final = jnp.einsum(
        "phdn,srn->psrhd", final_state.reshape(prompts, heads_loc, head_dim, state_dim), c_step,
        precision=lax.Precision.HIGHEST,
    )
    from_final = jnp.einsum("rp,psrhd->srhd", slot_pick, from_final, precision=lax.Precision.HIGHEST)
    overlap = jnp.einsum("trn,srn->tsr", b_step, c_step, precision=lax.Precision.HIGHEST)
    outputs = []
    carried = jnp.ones_like(step_decay[0])
    for step_index in range(steps):
        carried = carried * step_decay[step_index]
        y_step = carried[..., None] * from_final[step_index]
        for earlier in range(step_index + 1):
            weight = jnp.ones_like(step_decay[0])
            for later in range(earlier + 1, step_index + 1):
                weight = weight * step_decay[later]
            y_step = y_step + (weight * overlap[earlier, step_index][:, None])[..., None] * pushed[
                earlier
            ]
        y_step = y_step + skip[:, None] * x_step[step_index]
        gated_step = y_step.reshape(slot_count, inner_loc) * jax.nn.silu(
            step_z[step_index].astype(jnp.float32)
        )
        outputs.append(jnp.where(live_slots[:, None], gated_step, 0.0).astype(jnp.bfloat16))
    return (out, jnp.stack(outputs))

def solution(mesh):
    placed = (
        P("ctx", None, "head"),
        P("ctx", None, "head"),
        P("ctx", None, None),
        P("ctx", None, "head"),
        P("head"),
        P("head"),
        P("head"),
        P(None, "head"),
        P(),
        P("head"),
        P("head", None),
        P("ctx"),
        P(None, "ctx", "head"),
        P(None, "ctx", "head"),
        P(None, "ctx", None),
        P(None, "ctx", "head"),
    )
    return jax.shard_map(
        body,
        mesh=mesh,
        in_specs=placed,
        out_specs=(P(("ctx", "head"), None, None), P(None, "ctx", "head")),
        check_vma=False,
    )
```

```python
import jax
import jax.numpy as jnp
from jax import lax
from jax.sharding import PartitionSpec as P

norm_eps = 1e-05


def passed_along(value, axis, steps):
    count = lax.axis_size(axis)
    leading, last = (max(0, -steps), min(count, count - steps))
    return lax.ppermute(value, axis, [(source, source + steps) for source in range(leading, last)])


def group_shift(value, axis, count, stride, group, shift):
    pairs = []
    for source in range(count):
        member = (source // stride) % group
        target = source + (((member + shift) % group) - member) * stride
        pairs.append((source, target))
    return lax.ppermute(value, axis, pairs)


def conv_silu(window, weight, length):
    running_sum = jnp.zeros((length,) + window.shape[1:], jnp.float32)
    for offset in range(weight.shape[0]):
        running_sum = running_sum + window[offset : offset + length].astype(jnp.float32) * weight[
            offset
        ].astype(jnp.float32)
    return jax.nn.silu(running_sum).astype(jnp.bfloat16)


def chain(earlier, later):
    return (earlier[0] * later[0], later[0][..., None, None] * earlier[1] + later[1])


def pick(flag, first, second):
    return jax.tree.map(lambda a, b: jnp.where(flag, a, b), first, second)


def ring_scan(own, axis, count, stride, group):
    member = (lax.axis_index(axis) // stride) % group
    if group == 4:
        from_prev = group_shift(own, axis, count, stride, group, 1)
        from_next = group_shift(own, axis, count, stride, group, -1)
        split = own[1].shape[2] // 2
        lead = group_shift(
            (from_prev[0], from_prev[1][:, :, :split]), axis, count, stride, group, 1
        )
        rest = group_shift(from_next[1][:, :, split:], axis, count, stride, group, -1)
        far = (lead[0], jnp.concatenate([lead[1], rest], 2))
        received = [None, from_prev, far, from_next]
    else:
        received = [None] + [
            group_shift(own, axis, count, stride, group, shift) for shift in range(1, group)
        ]
    identity = (jnp.ones_like(own[0]), jnp.zeros_like(own[1]))
    before = identity
    for shift in range(group - 1, 0, -1):
        before = pick(shift <= member, chain(before, received[shift]), before)
    total = chain(before, own)
    for shift in range(group - 1, 0, -1):
        total = pick(shift > member, chain(total, received[shift]), total)
    return before, total


def body(
    x_in,
    z_in,
    bc_in,
    dt_in,
    dt_bias,
    a_log,
    skip,
    conv_x,
    conv_bc,
    norm_gain,
    w_out,
    requests,
    step_x,
    step_z,
    step_bc,
    step_dt,
):
    block_len, prompts, inner_loc = x_in.shape
    heads_loc = dt_in.shape[2]
    head_dim = inner_loc // heads_loc
    state_dim = bc_in.shape[2] // 2
    conv_taps = conv_x.shape[0]
    edge_x, edge_bc = passed_along(
        (x_in[block_len - conv_taps + 1 :], bc_in[block_len - conv_taps + 1 :]), "ctx", 1
    )
    x_conv = conv_silu(jnp.concatenate([edge_x, x_in], axis=0), conv_x, block_len)
    bc_conv = conv_silu(jnp.concatenate([edge_bc, bc_in], axis=0), conv_bc, block_len)
    b_rows = bc_conv[..., :state_dim]
    c_rows = bc_conv[..., state_dim:]
    decay_rates = -jnp.exp(a_log)
    dt_full = jax.nn.softplus(dt_in + dt_bias)
    cum_log = jnp.cumsum(dt_full * decay_rates, axis=0)
    cum_heads = jnp.transpose(cum_log, (1, 2, 0))
    dt_heads = jnp.transpose(dt_full, (1, 2, 0))
    x_heads = x_conv.reshape(block_len, prompts, heads_loc, head_dim)
    block_log = cum_heads[..., -1]
    tail_weights = jnp.transpose(jnp.exp(block_log[..., None] - cum_heads) * dt_heads, (2, 0, 1))
    weighted_x = (x_heads * tail_weights[..., None]).astype(jnp.bfloat16)
    s_local = jnp.einsum("jphd,jpn->phdn", weighted_x, b_rows, preferred_element_type=jnp.float32)
    block_decay = jnp.exp(block_log)

    count = lax.axis_size("ctx")
    here = lax.axis_index("ctx")
    core = here % 2
    tails = jax.tree.map(
        lambda part: lax.all_gather(part, "ctx")[count - 1],
        (x_in[block_len - conv_taps + 1 :], bc_in[block_len - conv_taps + 1 :]),
    )
    own = (block_decay, s_local)
    other = group_shift(own, "ctx", count, 1, 2, 1)
    first = pick(core == 0, own, other)
    second = pick(core == 0, other, own)
    chip_total = chain(first, second)
    half = head_dim // 2
    chip_half = (chip_total[0], lax.dynamic_slice_in_dim(chip_total[1], core * half, half, 2))
    row_before, row_total = ring_scan(chip_half, "ctx", count, 2, 4)
    rows = count // 8
    top_before, top_total = ring_scan(row_total, "ctx", count, 8, rows)
    chip_before = chain(top_before, row_before)
    mine = (chip_before[1], top_total[1])
    theirs = group_shift(mine, "ctx", count, 1, 2, 1)
    joined = jax.tree.map(
        lambda a, b: jnp.where(core == 0, jnp.concatenate([a, b], 2), jnp.concatenate([b, a], 2)),
        mine,
        theirs,
    )
    chip_state, final_state = joined
    s_before = jnp.where(
        core == 0, chip_state, first[0][..., None, None] * chip_state + first[1]
    )

    scores = jnp.einsum("ipn,jpn->pij", c_rows, b_rows, preferred_element_type=jnp.float32)
    position = lax.iota(jnp.int32, block_len)
    causal = position[:, None] >= position[None, :]
    gaps = jnp.where(causal, cum_heads[..., :, None] - cum_heads[..., None, :], -jnp.inf)
    mixing = (scores[:, None] * jnp.exp(gaps) * dt_heads[..., None, :]).astype(jnp.bfloat16)
    y_intra = jnp.einsum("phij,jphd->iphd", mixing, x_heads, preferred_element_type=jnp.float32)
    y_inter = (
        jnp.einsum(
            "ipn,phdn->iphd", c_rows.astype(jnp.float32), s_before, precision=lax.Precision.HIGHEST
        )
        * jnp.exp(cum_log)[..., None]
    )
    y_all = y_intra + y_inter + skip[:, None] * x_heads.astype(jnp.float32)
    gated_out = y_all.reshape(block_len, prompts, inner_loc) * jax.nn.silu(z_in.astype(jnp.float32))
    square_local = jnp.sum(gated_out * gated_out, axis=-1)
    head_count = lax.axis_size("head")
    square_sums = square_local
    for shift in range(1, head_count):
        square_sums = square_sums + group_shift(square_local, "head", head_count, 1, head_count, shift)
    inner_total = inner_loc * lax.axis_size("head")
    normed = (
        gated_out * lax.rsqrt(square_sums / inner_total + norm_eps)[..., None] * norm_gain
    ).astype(jnp.bfloat16)
    projected = lax.psum_scatter(
        jnp.einsum("tpi,id->tpd", normed, w_out, preferred_element_type=jnp.float32).astype(
            jnp.bfloat16
        ),
        "head",
        scatter_dimension=0,
        tiled=True,
    )
    out = projected.astype(jnp.bfloat16)

    final_x, final_bc = tails
    slot_count = requests.shape[0]
    steps = step_x.shape[0]
    slot_pick = (requests[:, None] == lax.iota(jnp.int32, prompts)[None, :]).astype(jnp.float32)
    live_slots = requests < prompts
    hist_x = jnp.einsum(
        "rp,kpi->kri", slot_pick, final_x.astype(jnp.float32), precision=lax.Precision.HIGHEST
    ).astype(jnp.bfloat16)
    hist_bc = jnp.einsum(
        "rp,kpi->kri", slot_pick, final_bc.astype(jnp.float32), precision=lax.Precision.HIGHEST
    ).astype(jnp.bfloat16)
    window_x = jnp.concatenate([hist_x, step_x], axis=0)
    window_bc = jnp.concatenate([hist_bc, step_bc], axis=0)
    new_x = conv_silu(window_x, conv_x, steps)
    new_bc = conv_silu(window_bc, conv_bc, steps)
    dt_step = jax.nn.softplus(step_dt + dt_bias)
    x_step = new_x.reshape(steps, slot_count, heads_loc, head_dim).astype(jnp.float32)
    b_step = new_bc[..., :state_dim].astype(jnp.float32)
    c_step = new_bc[..., state_dim:].astype(jnp.float32)
    step_decay = jnp.exp(dt_step * decay_rates)
    pushed = dt_step[..., None] * x_step
    from_final = jnp.einsum(
        "phdn,srn->psrhd", final_state.reshape(prompts, heads_loc, head_dim, state_dim), c_step,
        precision=lax.Precision.HIGHEST,
    )
    from_final = jnp.einsum("rp,psrhd->srhd", slot_pick, from_final, precision=lax.Precision.HIGHEST)
    overlap = jnp.einsum("trn,srn->tsr", b_step, c_step, precision=lax.Precision.HIGHEST)
    outputs = []
    carried = jnp.ones_like(step_decay[0])
    for step_index in range(steps):
        carried = carried * step_decay[step_index]
        y_step = carried[..., None] * from_final[step_index]
        for earlier in range(step_index + 1):
            weight = jnp.ones_like(step_decay[0])
            for later in range(earlier + 1, step_index + 1):
                weight = weight * step_decay[later]
            y_step = y_step + (weight * overlap[earlier, step_index][:, None])[..., None] * pushed[
                earlier
            ]
        y_step = y_step + skip[:, None] * x_step[step_index]
        gated_step = y_step.reshape(slot_count, inner_loc) * jax.nn.silu(
            step_z[step_index].astype(jnp.float32)
        )
        outputs.append(jnp.where(live_slots[:, None], gated_step, 0.0).astype(jnp.bfloat16))
    return (out, jnp.stack(outputs))

def solution(mesh):
    placed = (
        P("ctx", None, "head"),
        P("ctx", None, "head"),
        P("ctx", None, None),
        P("ctx", None, "head"),
        P("head"),
        P("head"),
        P("head"),
        P(None, "head"),
        P(),
        P("head"),
        P("head", None),
        P("ctx"),
        P(None, "ctx", "head"),
        P(None, "ctx", "head"),
        P(None, "ctx", None),
        P(None, "ctx", "head"),
    )
    return jax.shard_map(
        body,
        mesh=mesh,
        in_specs=placed,
        out_specs=(P(("ctx", "head"), None, None), P(None, "ctx", "head")),
        check_vma=False,
    )
```

```python
import jax
import jax.numpy as jnp
from jax import lax
from jax.sharding import PartitionSpec as P

norm_eps = 1e-05


def passed_along(value, axis, steps):
    count = lax.axis_size(axis)
    leading, last = (max(0, -steps), min(count, count - steps))
    return lax.ppermute(value, axis, [(source, source + steps) for source in range(leading, last)])


def group_shift(value, axis, count, stride, group, shift):
    pairs = []
    for source in range(count):
        member = (source // stride) % group
        target = source + (((member + shift) % group) - member) * stride
        pairs.append((source, target))
    return lax.ppermute(value, axis, pairs)


def conv_silu(window, weight, length):
    running_sum = jnp.zeros((length,) + window.shape[1:], jnp.float32)
    for offset in range(weight.shape[0]):
        running_sum = running_sum + window[offset : offset + length].astype(jnp.float32) * weight[
            offset
        ].astype(jnp.float32)
    return jax.nn.silu(running_sum).astype(jnp.bfloat16)


def chain(earlier, later):
    return (earlier[0] * later[0], later[0][..., None, None] * earlier[1] + later[1])


def pick(flag, first, second):
    return jax.tree.map(lambda a, b: jnp.where(flag, a, b), first, second)


def ring_scan(own, axis, count, stride, group):
    member = (lax.axis_index(axis) // stride) % group
    if group == 4:
        from_prev = group_shift(own, axis, count, stride, group, 1)
        from_next = group_shift(own, axis, count, stride, group, -1)
        split = own[1].shape[2] // 2
        lead = group_shift(
            (from_prev[0], from_prev[1][:, :, :split]), axis, count, stride, group, 1
        )
        rest = group_shift(from_next[1][:, :, split:], axis, count, stride, group, -1)
        far = (lead[0], jnp.concatenate([lead[1], rest], 2))
        received = [None, from_prev, far, from_next]
    else:
        received = [None] + [
            group_shift(own, axis, count, stride, group, shift) for shift in range(1, group)
        ]
    identity = (jnp.ones_like(own[0]), jnp.zeros_like(own[1]))
    before = identity
    for shift in range(group - 1, 0, -1):
        before = pick(shift <= member, chain(before, received[shift]), before)
    total = chain(before, own)
    for shift in range(group - 1, 0, -1):
        total = pick(shift > member, chain(total, received[shift]), total)
    return before, total


def body(
    x_in,
    z_in,
    bc_in,
    dt_in,
    dt_bias,
    a_log,
    skip,
    conv_x,
    conv_bc,
    norm_gain,
    w_out,
    requests,
    step_x,
    step_z,
    step_bc,
    step_dt,
):
    block_len, prompts, inner_loc = x_in.shape
    heads_loc = dt_in.shape[2]
    head_dim = inner_loc // heads_loc
    state_dim = bc_in.shape[2] // 2
    conv_taps = conv_x.shape[0]
    edge_x, edge_bc = passed_along(
        (x_in[block_len - conv_taps + 1 :], bc_in[block_len - conv_taps + 1 :]), "ctx", 1
    )
    x_conv = conv_silu(jnp.concatenate([edge_x, x_in], axis=0), conv_x, block_len)
    bc_conv = conv_silu(jnp.concatenate([edge_bc, bc_in], axis=0), conv_bc, block_len)
    b_rows = bc_conv[..., :state_dim]
    c_rows = bc_conv[..., state_dim:]
    decay_rates = -jnp.exp(a_log)
    dt_full = jax.nn.softplus(dt_in + dt_bias)
    cum_log = jnp.cumsum(dt_full * decay_rates, axis=0)
    cum_heads = jnp.transpose(cum_log, (1, 2, 0))
    dt_heads = jnp.transpose(dt_full, (1, 2, 0))
    x_heads = x_conv.reshape(block_len, prompts, heads_loc, head_dim)
    block_log = cum_heads[..., -1]
    tail_weights = jnp.transpose(jnp.exp(block_log[..., None] - cum_heads) * dt_heads, (2, 0, 1))
    weighted_x = (x_heads * tail_weights[..., None]).astype(jnp.bfloat16)
    s_local = jnp.einsum("jphd,jpn->phdn", weighted_x, b_rows, preferred_element_type=jnp.float32)
    block_decay = jnp.exp(block_log)

    count = lax.axis_size("ctx")
    here = lax.axis_index("ctx")
    core = here % 2
    tails = jax.tree.map(
        lambda part: lax.all_gather(part, "ctx")[count - 1],
        (x_in[block_len - conv_taps + 1 :], bc_in[block_len - conv_taps + 1 :]),
    )
    own = (block_decay, s_local)
    other = group_shift(own, "ctx", count, 1, 2, 1)
    first = pick(core == 0, own, other)
    second = pick(core == 0, other, own)
    chip_total = chain(first, second)
    half = head_dim // 2
    chip_half = (chip_total[0], lax.dynamic_slice_in_dim(chip_total[1], core * half, half, 2))
    row_before, row_total = ring_scan(chip_half, "ctx", count, 2, 4)
    rows = count // 8
    top_before, top_total = ring_scan(row_total, "ctx", count, 8, rows)
    chip_before = chain(top_before, row_before)
    mine = (chip_before[1], top_total[1])
    theirs = group_shift(mine, "ctx", count, 1, 2, 1)
    joined = jax.tree.map(
        lambda a, b: jnp.where(core == 0, jnp.concatenate([a, b], 2), jnp.concatenate([b, a], 2)),
        mine,
        theirs,
    )
    chip_state, final_state = joined
    s_before = jnp.where(
        core == 0, chip_state, first[0][..., None, None] * chip_state + first[1]
    )

    scores = jnp.einsum("ipn,jpn->pij", c_rows, b_rows, preferred_element_type=jnp.float32)
    position = lax.iota(jnp.int32, block_len)
    causal = position[:, None] >= position[None, :]
    gaps = jnp.where(causal, cum_heads[..., :, None] - cum_heads[..., None, :], -jnp.inf)
    mixing = (scores[:, None] * jnp.exp(gaps) * dt_heads[..., None, :]).astype(jnp.bfloat16)
    y_intra = jnp.einsum("phij,jphd->iphd", mixing, x_heads, preferred_element_type=jnp.float32)
    y_inter = (
        jnp.einsum(
            "ipn,phdn->iphd", c_rows.astype(jnp.float32), s_before, precision=lax.Precision.HIGHEST
        )
        * jnp.exp(cum_log)[..., None]
    )
    y_local = lax.optimization_barrier(y_intra + skip[:, None] * x_heads.astype(jnp.float32))
    y_all = y_local + y_inter
    gated_out = y_all.reshape(block_len, prompts, inner_loc) * jax.nn.silu(z_in.astype(jnp.float32))
    square_local = jnp.sum(gated_out * gated_out, axis=-1)
    head_count = lax.axis_size("head")
    square_sums = square_local
    for shift in range(1, head_count):
        square_sums = square_sums + group_shift(square_local, "head", head_count, 1, head_count, shift)
    inner_total = inner_loc * lax.axis_size("head")
    normed = (
        gated_out * lax.rsqrt(square_sums / inner_total + norm_eps)[..., None] * norm_gain
    ).astype(jnp.bfloat16)
    head_count = lax.axis_size("head")
    share = block_len // head_count
    halves = normed.reshape(head_count, 2, share // 2, prompts, inner_loc)
    out = jnp.concatenate(
        [
            lax.psum_scatter(
                jnp.einsum(
                    "tpi,id->tpd",
                    halves[:, part].reshape(block_len // 2, prompts, inner_loc),
                    w_out,
                    preferred_element_type=jnp.float32,
                ).astype(jnp.bfloat16),
                "head",
                scatter_dimension=0,
                tiled=True,
            )
            for part in range(2)
        ],
        axis=0,
    )

    final_x, final_bc = tails
    slot_count = requests.shape[0]
    steps = step_x.shape[0]
    slot_pick = (requests[:, None] == lax.iota(jnp.int32, prompts)[None, :]).astype(jnp.float32)
    live_slots = requests < prompts
    hist_x = jnp.einsum(
        "rp,kpi->kri", slot_pick, final_x.astype(jnp.float32), precision=lax.Precision.HIGHEST
    ).astype(jnp.bfloat16)
    hist_bc = jnp.einsum(
        "rp,kpi->kri", slot_pick, final_bc.astype(jnp.float32), precision=lax.Precision.HIGHEST
    ).astype(jnp.bfloat16)
    window_x = jnp.concatenate([hist_x, step_x], axis=0)
    window_bc = jnp.concatenate([hist_bc, step_bc], axis=0)
    new_x = conv_silu(window_x, conv_x, steps)
    new_bc = conv_silu(window_bc, conv_bc, steps)
    dt_step = jax.nn.softplus(step_dt + dt_bias)
    x_step = new_x.reshape(steps, slot_count, heads_loc, head_dim).astype(jnp.float32)
    b_step = new_bc[..., :state_dim].astype(jnp.float32)
    c_step = new_bc[..., state_dim:].astype(jnp.float32)
    step_log = jnp.cumsum(dt_step * decay_rates, axis=0)
    pushed = dt_step[..., None] * x_step
    from_final = jnp.einsum(
        "phdn,srn->psrhd", final_state.reshape(prompts, heads_loc, head_dim, state_dim), c_step,
        precision=lax.Precision.HIGHEST,
    )
    from_final = jnp.einsum("rp,psrhd->srhd", slot_pick, from_final, precision=lax.Precision.HIGHEST)
    overlap = jnp.einsum("trn,srn->tsr", b_step, c_step, precision=lax.Precision.HIGHEST)
    order = lax.iota(jnp.int32, steps)
    reach = (order[:, None] <= order[None, :])[..., None, None]
    gaps = jnp.where(reach, step_log[None, :] - step_log[:, None], -jnp.inf)
    weights = jnp.exp(gaps) * overlap[..., None]
    y_steps = (
        jnp.exp(step_log)[..., None] * from_final
        + jnp.einsum("tsrh,trhd->srhd", weights, pushed, precision=lax.Precision.HIGHEST)
        + skip[:, None] * x_step
    )
    gated_steps = y_steps.reshape(steps, slot_count, inner_loc) * jax.nn.silu(
        step_z.astype(jnp.float32)
    )
    dec_out = jnp.where(live_slots[None, :, None], gated_steps, 0.0).astype(jnp.bfloat16)
    return (out, dec_out)

def solution(mesh):
    placed = (
        P("ctx", None, "head"),
        P("ctx", None, "head"),
        P("ctx", None, None),
        P("ctx", None, "head"),
        P("head"),
        P("head"),
        P("head"),
        P(None, "head"),
        P(),
        P("head"),
        P("head", None),
        P("ctx"),
        P(None, "ctx", "head"),
        P(None, "ctx", "head"),
        P(None, "ctx", None),
        P(None, "ctx", "head"),
    )
    return jax.shard_map(
        body,
        mesh=mesh,
        in_specs=placed,
        out_specs=(P(("ctx", "head"), None, None), P(None, "ctx", "head")),
        check_vma=False,
    )
```

```python
import jax
import jax.numpy as jnp
from jax import lax
from jax.sharding import PartitionSpec as P

norm_eps = 1e-05


def passed_along(value, axis, steps):
    count = lax.axis_size(axis)
    leading, last = (max(0, -steps), min(count, count - steps))
    return lax.ppermute(value, axis, [(source, source + steps) for source in range(leading, last)])


def group_shift(value, axis, count, stride, group, shift):
    pairs = []
    for source in range(count):
        member = (source // stride) % group
        target = source + (((member + shift) % group) - member) * stride
        pairs.append((source, target))
    return lax.ppermute(value, axis, pairs)


def conv_silu(window, weight, length):
    running_sum = jnp.zeros((length,) + window.shape[1:], jnp.float32)
    for offset in range(weight.shape[0]):
        running_sum = running_sum + window[offset : offset + length].astype(jnp.float32) * weight[
            offset
        ].astype(jnp.float32)
    return jax.nn.silu(running_sum).astype(jnp.bfloat16)


def chain(earlier, later):
    return (earlier[0] * later[0], later[0][..., None, None] * earlier[1] + later[1])


def pick(flag, first, second):
    return jax.tree.map(lambda a, b: jnp.where(flag, a, b), first, second)


def ring_scan(own, axis, count, stride, group):
    member = (lax.axis_index(axis) // stride) % group
    if group == 4:
        from_prev = group_shift(own, axis, count, stride, group, 1)
        from_next = group_shift(own, axis, count, stride, group, -1)
        split = own[1].shape[2] // 2
        lead = group_shift(
            (from_prev[0], from_prev[1][:, :, :split]), axis, count, stride, group, 1
        )
        rest = group_shift(from_next[1][:, :, split:], axis, count, stride, group, -1)
        far = (lead[0], jnp.concatenate([lead[1], rest], 2))
        received = [None, from_prev, far, from_next]
    else:
        received = [None] + [
            group_shift(own, axis, count, stride, group, shift) for shift in range(1, group)
        ]
    identity = (jnp.ones_like(own[0]), jnp.zeros_like(own[1]))
    before = identity
    for shift in range(group - 1, 0, -1):
        before = pick(shift <= member, chain(before, received[shift]), before)
    total = chain(before, own)
    for shift in range(group - 1, 0, -1):
        total = pick(shift > member, chain(total, received[shift]), total)
    return before, total


def body(
    x_in,
    z_in,
    bc_in,
    dt_in,
    dt_bias,
    a_log,
    skip,
    conv_x,
    conv_bc,
    norm_gain,
    w_out,
    requests,
    step_x,
    step_z,
    step_bc,
    step_dt,
):
    block_len, prompts, inner_loc = x_in.shape
    heads_loc = dt_in.shape[2]
    head_dim = inner_loc // heads_loc
    state_dim = bc_in.shape[2] // 2
    conv_taps = conv_x.shape[0]
    edge_x, edge_bc = passed_along(
        (x_in[block_len - conv_taps + 1 :], bc_in[block_len - conv_taps + 1 :]), "ctx", 1
    )
    x_conv = conv_silu(jnp.concatenate([edge_x, x_in], axis=0), conv_x, block_len)
    bc_conv = conv_silu(jnp.concatenate([edge_bc, bc_in], axis=0), conv_bc, block_len)
    b_rows = bc_conv[..., :state_dim]
    c_rows = bc_conv[..., state_dim:]
    decay_rates = -jnp.exp(a_log)
    dt_full = jax.nn.softplus(dt_in + dt_bias)
    cum_log = jnp.cumsum(dt_full * decay_rates, axis=0)
    cum_heads = jnp.transpose(cum_log, (1, 2, 0))
    dt_heads = jnp.transpose(dt_full, (1, 2, 0))
    x_heads = x_conv.reshape(block_len, prompts, heads_loc, head_dim)
    block_log = cum_heads[..., -1]
    tail_weights = jnp.transpose(jnp.exp(block_log[..., None] - cum_heads) * dt_heads, (2, 0, 1))
    weighted_x = (x_heads * tail_weights[..., None]).astype(jnp.bfloat16)
    s_local = jnp.einsum("jphd,jpn->phdn", weighted_x, b_rows, preferred_element_type=jnp.float32)
    block_decay = jnp.exp(block_log)

    count = lax.axis_size("ctx")
    here = lax.axis_index("ctx")
    core = here % 2
    tails = (x_in[block_len - conv_taps + 1 :], bc_in[block_len - conv_taps + 1 :])
    reach = count // 2
    while reach >= 1:
        sent = lax.ppermute(
            tails,
            "ctx",
            [(source, source - reach) for source in range(count) if source % (2 * reach) == 2 * reach - 1],
        )
        taking = here % (2 * reach) == reach - 1
        tails = pick(taking, sent, tails)
        reach //= 2
    own = (block_decay, s_local)
    other = group_shift(own, "ctx", count, 1, 2, 1)
    first = pick(core == 0, own, other)
    second = pick(core == 0, other, own)
    chip_total = chain(first, second)
    half = head_dim // 2
    chip_half = (chip_total[0], lax.dynamic_slice_in_dim(chip_total[1], core * half, half, 2))
    row_before, row_total = ring_scan(chip_half, "ctx", count, 2, 4)
    rows = count // 8
    top_before, top_total = ring_scan(row_total, "ctx", count, 8, rows)
    chip_before = chain(top_before, row_before)
    mine = (chip_before[1], top_total[1])
    theirs = group_shift(mine, "ctx", count, 1, 2, 1)
    joined = jax.tree.map(
        lambda a, b: jnp.where(core == 0, jnp.concatenate([a, b], 2), jnp.concatenate([b, a], 2)),
        mine,
        theirs,
    )
    chip_state, final_state = joined
    s_before = jnp.where(
        core == 0, chip_state, first[0][..., None, None] * chip_state + first[1]
    )

    scores = jnp.einsum("ipn,jpn->pij", c_rows, b_rows, preferred_element_type=jnp.float32)
    position = lax.iota(jnp.int32, block_len)
    causal = position[:, None] >= position[None, :]
    gaps = jnp.where(causal, cum_heads[..., :, None] - cum_heads[..., None, :], -jnp.inf)
    mixing = (scores[:, None] * jnp.exp(gaps) * dt_heads[..., None, :]).astype(jnp.bfloat16)
    y_intra = jnp.einsum("phij,jphd->iphd", mixing, x_heads, preferred_element_type=jnp.float32)
    y_inter = (
        jnp.einsum(
            "ipn,phdn->iphd", c_rows.astype(jnp.float32), s_before, precision=lax.Precision.HIGHEST
        )
        * jnp.exp(cum_log)[..., None]
    )
    y_all = y_intra + y_inter + skip[:, None] * x_heads.astype(jnp.float32)
    gated_out = y_all.reshape(block_len, prompts, inner_loc) * jax.nn.silu(z_in.astype(jnp.float32))
    square_local = jnp.sum(gated_out * gated_out, axis=-1)
    head_count = lax.axis_size("head")
    square_sums = square_local
    for shift in range(1, head_count):
        square_sums = square_sums + group_shift(square_local, "head", head_count, 1, head_count, shift)
    inner_total = inner_loc * lax.axis_size("head")
    normed = (
        gated_out * lax.rsqrt(square_sums / inner_total + norm_eps)[..., None] * norm_gain
    ).astype(jnp.bfloat16)
    projected = lax.psum_scatter(
        jnp.einsum("tpi,id->tpd", normed, w_out, preferred_element_type=jnp.float32).astype(
            jnp.bfloat16
        ),
        "head",
        scatter_dimension=0,
        tiled=True,
    )
    out = projected.astype(jnp.bfloat16)

    final_x, final_bc = tails
    slot_count = requests.shape[0]
    steps = step_x.shape[0]
    slot_pick = (requests[:, None] == lax.iota(jnp.int32, prompts)[None, :]).astype(jnp.float32)
    live_slots = requests < prompts
    hist_x = jnp.einsum(
        "rp,kpi->kri", slot_pick, final_x.astype(jnp.float32), precision=lax.Precision.HIGHEST
    ).astype(jnp.bfloat16)
    hist_bc = jnp.einsum(
        "rp,kpi->kri", slot_pick, final_bc.astype(jnp.float32), precision=lax.Precision.HIGHEST
    ).astype(jnp.bfloat16)
    window_x = jnp.concatenate([hist_x, step_x], axis=0)
    window_bc = jnp.concatenate([hist_bc, step_bc], axis=0)
    new_x = conv_silu(window_x, conv_x, steps)
    new_bc = conv_silu(window_bc, conv_bc, steps)
    dt_step = jax.nn.softplus(step_dt + dt_bias)
    x_step = new_x.reshape(steps, slot_count, heads_loc, head_dim).astype(jnp.float32)
    b_step = new_bc[..., :state_dim].astype(jnp.float32)
    c_step = new_bc[..., state_dim:].astype(jnp.float32)
    step_decay = jnp.exp(dt_step * decay_rates)
    pushed = dt_step[..., None] * x_step
    from_final = jnp.einsum(
        "phdn,srn->psrhd", final_state.reshape(prompts, heads_loc, head_dim, state_dim), c_step,
        precision=lax.Precision.HIGHEST,
    )
    from_final = jnp.einsum("rp,psrhd->srhd", slot_pick, from_final, precision=lax.Precision.HIGHEST)
    overlap = jnp.einsum("trn,srn->tsr", b_step, c_step, precision=lax.Precision.HIGHEST)
    outputs = []
    carried = jnp.ones_like(step_decay[0])
    for step_index in range(steps):
        carried = carried * step_decay[step_index]
        y_step = carried[..., None] * from_final[step_index]
        for earlier in range(step_index + 1):
            weight = jnp.ones_like(step_decay[0])
            for later in range(earlier + 1, step_index + 1):
                weight = weight * step_decay[later]
            y_step = y_step + (weight * overlap[earlier, step_index][:, None])[..., None] * pushed[
                earlier
            ]
        y_step = y_step + skip[:, None] * x_step[step_index]
        gated_step = y_step.reshape(slot_count, inner_loc) * jax.nn.silu(
            step_z[step_index].astype(jnp.float32)
        )
        outputs.append(jnp.where(live_slots[:, None], gated_step, 0.0).astype(jnp.bfloat16))
    return (out, jnp.stack(outputs))

def solution(mesh):
    placed = (
        P("ctx", None, "head"),
        P("ctx", None, "head"),
        P("ctx", None, None),
        P("ctx", None, "head"),
        P("head"),
        P("head"),
        P("head"),
        P(None, "head"),
        P(),
        P("head"),
        P("head", None),
        P("ctx"),
        P(None, "ctx", "head"),
        P(None, "ctx", "head"),
        P(None, "ctx", None),
        P(None, "ctx", "head"),
    )
    return jax.shard_map(
        body,
        mesh=mesh,
        in_specs=placed,
        out_specs=(P(("ctx", "head"), None, None), P(None, "ctx", "head")),
        check_vma=False,
    )
```

```python
import jax
import jax.numpy as jnp
from jax import lax
from jax.sharding import PartitionSpec as P

norm_eps = 1e-05


def passed_along(value, axis, steps):
    count = lax.axis_size(axis)
    leading, last = (max(0, -steps), min(count, count - steps))
    return lax.ppermute(value, axis, [(source, source + steps) for source in range(leading, last)])


def group_shift(value, axis, count, stride, group, shift):
    pairs = []
    for source in range(count):
        member = (source // stride) % group
        target = source + (((member + shift) % group) - member) * stride
        pairs.append((source, target))
    return lax.ppermute(value, axis, pairs)


def conv_silu(window, weight, length):
    running_sum = jnp.zeros((length,) + window.shape[1:], jnp.float32)
    for offset in range(weight.shape[0]):
        running_sum = running_sum + window[offset : offset + length].astype(jnp.float32) * weight[
            offset
        ].astype(jnp.float32)
    return jax.nn.silu(running_sum).astype(jnp.bfloat16)


def chain(earlier, later):
    return (earlier[0] * later[0], later[0][..., None, None] * earlier[1] + later[1])


def pick(flag, first, second):
    return jax.tree.map(lambda a, b: jnp.where(flag, a, b), first, second)


def ring_scan(own, axis, count, stride, group):
    member = (lax.axis_index(axis) // stride) % group
    if group == 4:
        from_prev = group_shift(own, axis, count, stride, group, 1)
        from_next = group_shift(own, axis, count, stride, group, -1)
        split = own[1].shape[2] // 2
        lead = group_shift(
            (from_prev[0], from_prev[1][:, :, :split]), axis, count, stride, group, 1
        )
        rest = group_shift(from_next[1][:, :, split:], axis, count, stride, group, -1)
        far = (lead[0], jnp.concatenate([lead[1], rest], 2))
        received = [None, from_prev, far, from_next]
    else:
        received = [None] + [
            group_shift(own, axis, count, stride, group, shift) for shift in range(1, group)
        ]
    identity = (jnp.ones_like(own[0]), jnp.zeros_like(own[1]))
    before = identity
    for shift in range(group - 1, 0, -1):
        before = pick(shift <= member, chain(before, received[shift]), before)
    total = chain(before, own)
    for shift in range(group - 1, 0, -1):
        total = pick(shift > member, chain(total, received[shift]), total)
    return before, total


def ring_reduce_scatter(part, axis):
    count = lax.axis_size(axis)
    here = lax.axis_index(axis)
    share = part.shape[0] // count
    split = part.shape[2] // 2

    def chunk(offset):
        return lax.dynamic_slice_in_dim(part, ((here + offset) % count) * share, share, 0)

    def passed(value, shift):
        return group_shift(value.astype(jnp.bfloat16), axis, count, 1, count, shift).astype(
            jnp.float32
        )

    forward = chunk(-1)[..., :split]
    backward = chunk(1)[..., split:]
    for step in range(2, count):
        forward = passed(forward, 1) + chunk(-step)[..., :split]
        backward = passed(backward, -1) + chunk(step)[..., split:]
    own = chunk(0)
    forward = passed(forward, 1) + own[..., :split]
    backward = passed(backward, -1) + own[..., split:]
    return jnp.concatenate([forward, backward], axis=2)


def body(
    x_in,
    z_in,
    bc_in,
    dt_in,
    dt_bias,
    a_log,
    skip,
    conv_x,
    conv_bc,
    norm_gain,
    w_out,
    requests,
    step_x,
    step_z,
    step_bc,
    step_dt,
):
    block_len, prompts, inner_loc = x_in.shape
    heads_loc = dt_in.shape[2]
    head_dim = inner_loc // heads_loc
    state_dim = bc_in.shape[2] // 2
    conv_taps = conv_x.shape[0]
    edge_x, edge_bc = passed_along(
        (x_in[block_len - conv_taps + 1 :], bc_in[block_len - conv_taps + 1 :]), "ctx", 1
    )
    x_conv = conv_silu(jnp.concatenate([edge_x, x_in], axis=0), conv_x, block_len)
    bc_conv = conv_silu(jnp.concatenate([edge_bc, bc_in], axis=0), conv_bc, block_len)
    b_rows = bc_conv[..., :state_dim]
    c_rows = bc_conv[..., state_dim:]
    decay_rates = -jnp.exp(a_log)
    dt_full = jax.nn.softplus(dt_in + dt_bias)
    cum_log = jnp.cumsum(dt_full * decay_rates, axis=0)
    cum_heads = jnp.transpose(cum_log, (1, 2, 0))
    dt_heads = jnp.transpose(dt_full, (1, 2, 0))
    x_heads = x_conv.reshape(block_len, prompts, heads_loc, head_dim)
    block_log = cum_heads[..., -1]
    tail_weights = jnp.transpose(jnp.exp(block_log[..., None] - cum_heads) * dt_heads, (2, 0, 1))
    weighted_x = (x_heads * tail_weights[..., None]).astype(jnp.bfloat16)
    s_local = jnp.einsum("jphd,jpn->phdn", weighted_x, b_rows, preferred_element_type=jnp.float32)
    block_decay = jnp.exp(block_log)

    count = lax.axis_size("ctx")
    here = lax.axis_index("ctx")
    core = here % 2
    tails = (x_in[block_len - conv_taps + 1 :], bc_in[block_len - conv_taps + 1 :])
    reach = count // 2
    while reach >= 1:
        sent = lax.ppermute(
            tails,
            "ctx",
            [(source, source - reach) for source in range(count) if source % (2 * reach) == 2 * reach - 1],
        )
        taking = here % (2 * reach) == reach - 1
        tails = pick(taking, sent, tails)
        reach //= 2
    own = (block_decay, s_local)
    other = group_shift(own, "ctx", count, 1, 2, 1)
    first = pick(core == 0, own, other)
    second = pick(core == 0, other, own)
    chip_total = chain(first, second)
    half = head_dim // 2
    chip_half = (chip_total[0], lax.dynamic_slice_in_dim(chip_total[1], core * half, half, 2))
    row_before, row_total = ring_scan(chip_half, "ctx", count, 2, 4)
    rows = count // 8
    top_before, top_total = ring_scan(row_total, "ctx", count, 8, rows)
    chip_before = chain(top_before, row_before)
    mine = (chip_before[1], top_total[1])
    theirs = group_shift(mine, "ctx", count, 1, 2, 1)
    joined = jax.tree.map(
        lambda a, b: jnp.where(core == 0, jnp.concatenate([a, b], 2), jnp.concatenate([b, a], 2)),
        mine,
        theirs,
    )
    chip_state, final_state = joined
    s_before = jnp.where(
        core == 0, chip_state, first[0][..., None, None] * chip_state + first[1]
    )

    scores = jnp.einsum("ipn,jpn->pij", c_rows, b_rows, preferred_element_type=jnp.float32)
    position = lax.iota(jnp.int32, block_len)
    causal = position[:, None] >= position[None, :]
    gaps = jnp.where(causal, cum_heads[..., :, None] - cum_heads[..., None, :], -jnp.inf)
    mixing = (scores[:, None] * jnp.exp(gaps) * dt_heads[..., None, :]).astype(jnp.bfloat16)
    y_intra = jnp.einsum("phij,jphd->iphd", mixing, x_heads, preferred_element_type=jnp.float32)
    y_inter = (
        jnp.einsum(
            "ipn,phdn->iphd", c_rows.astype(jnp.float32), s_before, precision=lax.Precision.HIGHEST
        )
        * jnp.exp(cum_log)[..., None]
    )
    y_all = y_intra + y_inter + skip[:, None] * x_heads.astype(jnp.float32)
    gated_out = y_all.reshape(block_len, prompts, inner_loc) * jax.nn.silu(z_in.astype(jnp.float32))
    square_local = jnp.sum(gated_out * gated_out, axis=-1)
    head_count = lax.axis_size("head")
    square_sums = square_local
    for shift in range(1, head_count):
        square_sums = square_sums + group_shift(square_local, "head", head_count, 1, head_count, shift)
    inner_total = inner_loc * lax.axis_size("head")
    normed = (
        gated_out * lax.rsqrt(square_sums / inner_total + norm_eps)[..., None] * norm_gain
    ).astype(jnp.bfloat16)
    projected = jnp.einsum("tpi,id->tpd", normed, w_out, preferred_element_type=jnp.float32)
    out = ring_reduce_scatter(projected, "head").astype(jnp.bfloat16)

    final_x, final_bc = tails
    slot_count = requests.shape[0]
    steps = step_x.shape[0]
    slot_pick = (requests[:, None] == lax.iota(jnp.int32, prompts)[None, :]).astype(jnp.float32)
    live_slots = requests < prompts
    hist_x = jnp.einsum(
        "rp,kpi->kri", slot_pick, final_x.astype(jnp.float32), precision=lax.Precision.HIGHEST
    ).astype(jnp.bfloat16)
    hist_bc = jnp.einsum(
        "rp,kpi->kri", slot_pick, final_bc.astype(jnp.float32), precision=lax.Precision.HIGHEST
    ).astype(jnp.bfloat16)
    window_x = jnp.concatenate([hist_x, step_x], axis=0)
    window_bc = jnp.concatenate([hist_bc, step_bc], axis=0)
    new_x = conv_silu(window_x, conv_x, steps)
    new_bc = conv_silu(window_bc, conv_bc, steps)
    dt_step = jax.nn.softplus(step_dt + dt_bias)
    x_step = new_x.reshape(steps, slot_count, heads_loc, head_dim).astype(jnp.float32)
    b_step = new_bc[..., :state_dim].astype(jnp.float32)
    c_step = new_bc[..., state_dim:].astype(jnp.float32)
    step_decay = jnp.exp(dt_step * decay_rates)
    pushed = dt_step[..., None] * x_step
    from_final = jnp.einsum(
        "phdn,srn->psrhd", final_state.reshape(prompts, heads_loc, head_dim, state_dim), c_step,
        precision=lax.Precision.HIGHEST,
    )
    from_final = jnp.einsum("rp,psrhd->srhd", slot_pick, from_final, precision=lax.Precision.HIGHEST)
    overlap = jnp.einsum("trn,srn->tsr", b_step, c_step, precision=lax.Precision.HIGHEST)
    outputs = []
    carried = jnp.ones_like(step_decay[0])
    for step_index in range(steps):
        carried = carried * step_decay[step_index]
        y_step = carried[..., None] * from_final[step_index]
        for earlier in range(step_index + 1):
            weight = jnp.ones_like(step_decay[0])
            for later in range(earlier + 1, step_index + 1):
                weight = weight * step_decay[later]
            y_step = y_step + (weight * overlap[earlier, step_index][:, None])[..., None] * pushed[
                earlier
            ]
        y_step = y_step + skip[:, None] * x_step[step_index]
        gated_step = y_step.reshape(slot_count, inner_loc) * jax.nn.silu(
            step_z[step_index].astype(jnp.float32)
        )
        outputs.append(jnp.where(live_slots[:, None], gated_step, 0.0).astype(jnp.bfloat16))
    return (out, jnp.stack(outputs))

def solution(mesh):
    placed = (
        P("ctx", None, "head"),
        P("ctx", None, "head"),
        P("ctx", None, None),
        P("ctx", None, "head"),
        P("head"),
        P("head"),
        P("head"),
        P(None, "head"),
        P(),
        P("head"),
        P("head", None),
        P("ctx"),
        P(None, "ctx", "head"),
        P(None, "ctx", "head"),
        P(None, "ctx", None),
        P(None, "ctx", "head"),
    )
    return jax.shard_map(
        body,
        mesh=mesh,
        in_specs=placed,
        out_specs=(P(("ctx", "head"), None, None), P(None, "ctx", "head")),
        check_vma=False,
    )
```

```python
import jax
import jax.numpy as jnp
from jax import lax
from jax.sharding import PartitionSpec as P

norm_eps = 1e-05


def passed_along(value, axis, steps):
    count = lax.axis_size(axis)
    leading, last = (max(0, -steps), min(count, count - steps))
    return lax.ppermute(value, axis, [(source, source + steps) for source in range(leading, last)])


def group_shift(value, axis, count, stride, group, shift):
    pairs = []
    for source in range(count):
        member = (source // stride) % group
        target = source + (((member + shift) % group) - member) * stride
        pairs.append((source, target))
    return lax.ppermute(value, axis, pairs)


def conv_silu(window, weight, length):
    running_sum = jnp.zeros((length,) + window.shape[1:], jnp.float32)
    for offset in range(weight.shape[0]):
        running_sum = running_sum + window[offset : offset + length].astype(jnp.float32) * weight[
            offset
        ].astype(jnp.float32)
    return jax.nn.silu(running_sum).astype(jnp.bfloat16)


def chain(earlier, later):
    return (earlier[0] * later[0], later[0][..., None, None] * earlier[1] + later[1])


def pick(flag, first, second):
    return jax.tree.map(lambda a, b: jnp.where(flag, a, b), first, second)


def ring_scan(own, axis, count, stride, group):
    member = (lax.axis_index(axis) // stride) % group
    if group == 4:
        from_prev = group_shift(own, axis, count, stride, group, 1)
        from_next = group_shift(own, axis, count, stride, group, -1)
        split = own[1].shape[2] // 2
        lead = group_shift(
            (from_prev[0], from_prev[1][:, :, :split]), axis, count, stride, group, 1
        )
        rest = group_shift(from_next[1][:, :, split:], axis, count, stride, group, -1)
        far = (lead[0], jnp.concatenate([lead[1], rest], 2))
        received = [None, from_prev, far, from_next]
    else:
        received = [None] + [
            group_shift(own, axis, count, stride, group, shift) for shift in range(1, group)
        ]
    identity = (jnp.ones_like(own[0]), jnp.zeros_like(own[1]))
    before = identity
    for shift in range(group - 1, 0, -1):
        before = pick(shift <= member, chain(before, received[shift]), before)
    total = chain(before, own)
    for shift in range(group - 1, 0, -1):
        total = pick(shift > member, chain(total, received[shift]), total)
    return before, total


def ring_reduce_scatter(part, axis):
    count = lax.axis_size(axis)
    here = lax.axis_index(axis)
    share = part.shape[0] // count
    split = part.shape[2] // 2

    def chunk(offset):
        return lax.dynamic_slice_in_dim(part, ((here + offset) % count) * share, share, 0)

    def passed(value, shift):
        return group_shift(value.astype(jnp.bfloat16), axis, count, 1, count, shift).astype(
            jnp.float32
        )

    forward = chunk(-1)[..., :split]
    backward = chunk(1)[..., split:]
    for step in range(2, count):
        forward = passed(forward, 1) + chunk(-step)[..., :split]
        backward = passed(backward, -1) + chunk(step)[..., split:]
    own = chunk(0)
    forward = passed(forward, 1) + own[..., :split]
    backward = passed(backward, -1) + own[..., split:]
    return jnp.concatenate([forward, backward], axis=2)


def body(
    x_in,
    z_in,
    bc_in,
    dt_in,
    dt_bias,
    a_log,
    skip,
    conv_x,
    conv_bc,
    norm_gain,
    w_out,
    requests,
    step_x,
    step_z,
    step_bc,
    step_dt,
):
    block_len, prompts, inner_loc = x_in.shape
    heads_loc = dt_in.shape[2]
    head_dim = inner_loc // heads_loc
    state_dim = bc_in.shape[2] // 2
    conv_taps = conv_x.shape[0]
    edge_x, edge_bc = passed_along(
        (x_in[block_len - conv_taps + 1 :], bc_in[block_len - conv_taps + 1 :]), "ctx", 1
    )
    x_conv = conv_silu(jnp.concatenate([edge_x, x_in], axis=0), conv_x, block_len)
    bc_conv = conv_silu(jnp.concatenate([edge_bc, bc_in], axis=0), conv_bc, block_len)
    b_rows = bc_conv[..., :state_dim]
    c_rows = bc_conv[..., state_dim:]
    decay_rates = -jnp.exp(a_log)
    dt_full = jax.nn.softplus(dt_in + dt_bias)
    cum_log = jnp.cumsum(dt_full * decay_rates, axis=0)
    cum_heads = jnp.transpose(cum_log, (1, 2, 0))
    dt_heads = jnp.transpose(dt_full, (1, 2, 0))
    x_heads = x_conv.reshape(block_len, prompts, heads_loc, head_dim)
    block_log = cum_heads[..., -1]
    tail_weights = jnp.transpose(jnp.exp(block_log[..., None] - cum_heads) * dt_heads, (2, 0, 1))
    weighted_x = (x_heads * tail_weights[..., None]).astype(jnp.bfloat16)
    s_local = jnp.einsum("jphd,jpn->phdn", weighted_x, b_rows, preferred_element_type=jnp.float32)
    block_decay = jnp.exp(block_log)

    count = lax.axis_size("ctx")
    here = lax.axis_index("ctx")
    core = here % 2
    tails = (x_in[block_len - conv_taps + 1 :], bc_in[block_len - conv_taps + 1 :])
    sent = lax.ppermute(tails, "ctx", [(count - 1, count - 2)])
    tails = pick(here == count - 2, sent, tails)
    for shift in range(1, 4):
        sent = lax.ppermute(
            tails, "ctx", [(count - 2 + c, count - 2 + c - 2 * shift) for c in range(2)]
        )
        tails = pick((here >= count - 8) & ((here % 8) // 2 == 3 - shift), sent, tails)
    rows = count // 8
    for shift in range(1, rows):
        sent = lax.ppermute(
            tails, "ctx", [(count - 8 + j, count - 8 + j - 8 * shift) for j in range(8)]
        )
        tails = pick(here // 8 == rows - 1 - shift, sent, tails)
    own = (block_decay, s_local)
    other = group_shift(own, "ctx", count, 1, 2, 1)
    first = pick(core == 0, own, other)
    second = pick(core == 0, other, own)
    chip_total = chain(first, second)
    half = head_dim // 2
    chip_half = (chip_total[0], lax.dynamic_slice_in_dim(chip_total[1], core * half, half, 2))
    row_before, row_total = ring_scan(chip_half, "ctx", count, 2, 4)
    rows = count // 8
    top_before, top_total = ring_scan(row_total, "ctx", count, 8, rows)
    chip_before = chain(top_before, row_before)
    mine = (chip_before[1], top_total[1])
    theirs = group_shift(mine, "ctx", count, 1, 2, 1)
    joined = jax.tree.map(
        lambda a, b: jnp.where(core == 0, jnp.concatenate([a, b], 2), jnp.concatenate([b, a], 2)),
        mine,
        theirs,
    )
    chip_state, final_state = joined
    s_before = jnp.where(
        core == 0, chip_state, first[0][..., None, None] * chip_state + first[1]
    )

    scores = jnp.einsum("ipn,jpn->pij", c_rows, b_rows, preferred_element_type=jnp.float32)
    position = lax.iota(jnp.int32, block_len)
    causal = position[:, None] >= position[None, :]
    gaps = jnp.where(causal, cum_heads[..., :, None] - cum_heads[..., None, :], -jnp.inf)
    mixing = (scores[:, None] * jnp.exp(gaps) * dt_heads[..., None, :]).astype(jnp.bfloat16)
    y_intra = jnp.einsum("phij,jphd->iphd", mixing, x_heads, preferred_element_type=jnp.float32)
    y_inter = (
        jnp.einsum(
            "ipn,phdn->iphd", c_rows.astype(jnp.float32), s_before, precision=lax.Precision.HIGHEST
        )
        * jnp.exp(cum_log)[..., None]
    )
    y_all = y_intra + y_inter + skip[:, None] * x_heads.astype(jnp.float32)
    gated_out = y_all.reshape(block_len, prompts, inner_loc) * jax.nn.silu(z_in.astype(jnp.float32))
    square_local = jnp.sum(gated_out * gated_out, axis=-1)
    head_count = lax.axis_size("head")
    square_sums = square_local
    for shift in range(1, head_count):
        square_sums = square_sums + group_shift(square_local, "head", head_count, 1, head_count, shift)
    inner_total = inner_loc * lax.axis_size("head")
    normed = (
        gated_out * lax.rsqrt(square_sums / inner_total + norm_eps)[..., None] * norm_gain
    ).astype(jnp.bfloat16)
    projected = jnp.einsum("tpi,id->tpd", normed, w_out, preferred_element_type=jnp.float32)
    out = ring_reduce_scatter(projected, "head").astype(jnp.bfloat16)

    final_x, final_bc = tails
    slot_count = requests.shape[0]
    steps = step_x.shape[0]
    slot_pick = (requests[:, None] == lax.iota(jnp.int32, prompts)[None, :]).astype(jnp.float32)
    live_slots = requests < prompts
    hist_x = jnp.einsum(
        "rp,kpi->kri", slot_pick, final_x.astype(jnp.float32), precision=lax.Precision.HIGHEST
    ).astype(jnp.bfloat16)
    hist_bc = jnp.einsum(
        "rp,kpi->kri", slot_pick, final_bc.astype(jnp.float32), precision=lax.Precision.HIGHEST
    ).astype(jnp.bfloat16)
    window_x = jnp.concatenate([hist_x, step_x], axis=0)
    window_bc = jnp.concatenate([hist_bc, step_bc], axis=0)
    new_x = conv_silu(window_x, conv_x, steps)
    new_bc = conv_silu(window_bc, conv_bc, steps)
    dt_step = jax.nn.softplus(step_dt + dt_bias)
    x_step = new_x.reshape(steps, slot_count, heads_loc, head_dim).astype(jnp.float32)
    b_step = new_bc[..., :state_dim].astype(jnp.float32)
    c_step = new_bc[..., state_dim:].astype(jnp.float32)
    step_decay = jnp.exp(dt_step * decay_rates)
    pushed = dt_step[..., None] * x_step
    from_final = jnp.einsum(
        "phdn,srn->psrhd", final_state.reshape(prompts, heads_loc, head_dim, state_dim), c_step,
        precision=lax.Precision.HIGHEST,
    )
    from_final = jnp.einsum("rp,psrhd->srhd", slot_pick, from_final, precision=lax.Precision.HIGHEST)
    overlap = jnp.einsum("trn,srn->tsr", b_step, c_step, precision=lax.Precision.HIGHEST)
    outputs = []
    carried = jnp.ones_like(step_decay[0])
    for step_index in range(steps):
        carried = carried * step_decay[step_index]
        y_step = carried[..., None] * from_final[step_index]
        for earlier in range(step_index + 1):
            weight = jnp.ones_like(step_decay[0])
            for later in range(earlier + 1, step_index + 1):
                weight = weight * step_decay[later]
            y_step = y_step + (weight * overlap[earlier, step_index][:, None])[..., None] * pushed[
                earlier
            ]
        y_step = y_step + skip[:, None] * x_step[step_index]
        gated_step = y_step.reshape(slot_count, inner_loc) * jax.nn.silu(
            step_z[step_index].astype(jnp.float32)
        )
        outputs.append(jnp.where(live_slots[:, None], gated_step, 0.0).astype(jnp.bfloat16))
    return (out, jnp.stack(outputs))

def solution(mesh):
    placed = (
        P("ctx", None, "head"),
        P("ctx", None, "head"),
        P("ctx", None, None),
        P("ctx", None, "head"),
        P("head"),
        P("head"),
        P("head"),
        P(None, "head"),
        P(),
        P("head"),
        P("head", None),
        P("ctx"),
        P(None, "ctx", "head"),
        P(None, "ctx", "head"),
        P(None, "ctx", None),
        P(None, "ctx", "head"),
    )
    return jax.shard_map(
        body,
        mesh=mesh,
        in_specs=placed,
        out_specs=(P(("ctx", "head"), None, None), P(None, "ctx", "head")),
        check_vma=False,
    )
```

```python
import jax
import jax.numpy as jnp
from jax import lax
from jax.sharding import PartitionSpec as P

norm_eps = 1e-05


def passed_along(value, axis, steps):
    count = lax.axis_size(axis)
    leading, last = (max(0, -steps), min(count, count - steps))
    return lax.ppermute(value, axis, [(source, source + steps) for source in range(leading, last)])


def group_shift(value, axis, count, stride, group, shift):
    pairs = []
    for source in range(count):
        member = (source // stride) % group
        target = source + (((member + shift) % group) - member) * stride
        pairs.append((source, target))
    return lax.ppermute(value, axis, pairs)


def conv_silu(window, weight, length):
    running_sum = jnp.zeros((length,) + window.shape[1:], jnp.float32)
    for offset in range(weight.shape[0]):
        running_sum = running_sum + window[offset : offset + length].astype(jnp.float32) * weight[
            offset
        ].astype(jnp.float32)
    return jax.nn.silu(running_sum).astype(jnp.bfloat16)


def chain(earlier, later):
    return (earlier[0] * later[0], later[0][..., None, None] * earlier[1] + later[1])


def pick(flag, first, second):
    return jax.tree.map(lambda a, b: jnp.where(flag, a, b), first, second)


def ring_scan(own, axis, count, stride, group):
    member = (lax.axis_index(axis) // stride) % group
    if group == 4:
        from_prev = group_shift(own, axis, count, stride, group, 1)
        from_next = group_shift(own, axis, count, stride, group, -1)
        split = own[1].shape[2] // 2
        lead = group_shift(
            (from_prev[0], from_prev[1][:, :, :split]), axis, count, stride, group, 1
        )
        rest = group_shift(from_next[1][:, :, split:], axis, count, stride, group, -1)
        far = (lead[0], jnp.concatenate([lead[1], rest], 2))
        received = [None, from_prev, far, from_next]
    else:
        received = [None] + [
            group_shift(own, axis, count, stride, group, shift) for shift in range(1, group)
        ]
    identity = (jnp.ones_like(own[0]), jnp.zeros_like(own[1]))
    before = identity
    for shift in range(group - 1, 0, -1):
        before = pick(shift <= member, chain(before, received[shift]), before)
    total = chain(before, own)
    for shift in range(group - 1, 0, -1):
        total = pick(shift > member, chain(total, received[shift]), total)
    return before, total


def ring_reduce_scatter(part, axis):
    count = lax.axis_size(axis)
    here = lax.axis_index(axis)
    share = part.shape[0] // count
    split = part.shape[2] // 2

    def chunk(offset):
        return lax.dynamic_slice_in_dim(part, ((here + offset) % count) * share, share, 0)

    def passed(value, shift):
        return group_shift(value.astype(jnp.bfloat16), axis, count, 1, count, shift).astype(
            jnp.float32
        )

    forward = chunk(-1)[..., :split]
    backward = chunk(1)[..., split:]
    for step in range(2, count):
        forward = passed(forward, 1) + chunk(-step)[..., :split]
        backward = passed(backward, -1) + chunk(step)[..., split:]
    own = chunk(0)
    forward = passed(forward, 1) + own[..., :split]
    backward = passed(backward, -1) + own[..., split:]
    return jnp.concatenate([forward, backward], axis=2)


def body(
    x_in,
    z_in,
    bc_in,
    dt_in,
    dt_bias,
    a_log,
    skip,
    conv_x,
    conv_bc,
    norm_gain,
    w_out,
    requests,
    step_x,
    step_z,
    step_bc,
    step_dt,
):
    block_len, prompts, inner_loc = x_in.shape
    heads_loc = dt_in.shape[2]
    head_dim = inner_loc // heads_loc
    state_dim = bc_in.shape[2] // 2
    conv_taps = conv_x.shape[0]
    edge_x, edge_bc = passed_along(
        (x_in[block_len - conv_taps + 1 :], bc_in[block_len - conv_taps + 1 :]), "ctx", 1
    )
    x_conv = conv_silu(jnp.concatenate([edge_x, x_in], axis=0), conv_x, block_len)
    bc_conv = conv_silu(jnp.concatenate([edge_bc, bc_in], axis=0), conv_bc, block_len)
    b_rows = bc_conv[..., :state_dim]
    c_rows = bc_conv[..., state_dim:]
    decay_rates = -jnp.exp(a_log)
    dt_full = jax.nn.softplus(dt_in + dt_bias)
    cum_log = jnp.cumsum(dt_full * decay_rates, axis=0)
    cum_heads = jnp.transpose(cum_log, (1, 2, 0))
    dt_heads = jnp.transpose(dt_full, (1, 2, 0))
    x_heads = x_conv.reshape(block_len, prompts, heads_loc, head_dim)
    block_log = cum_heads[..., -1]
    tail_weights = jnp.transpose(jnp.exp(block_log[..., None] - cum_heads) * dt_heads, (2, 0, 1))
    weighted_x = (x_heads * tail_weights[..., None]).astype(jnp.bfloat16)
    s_local = jnp.einsum("jphd,jpn->phdn", weighted_x, b_rows, preferred_element_type=jnp.float32)
    block_decay = jnp.exp(block_log)

    count = lax.axis_size("ctx")
    here = lax.axis_index("ctx")
    core = here % 2
    tails = (x_in[block_len - conv_taps + 1 :], bc_in[block_len - conv_taps + 1 :])
    own = (block_decay, s_local)
    other = group_shift(own, "ctx", count, 1, 2, 1)
    first = pick(core == 0, own, other)
    second = pick(core == 0, other, own)
    chip_total = chain(first, second)
    half = head_dim // 2
    chip_half = (chip_total[0], lax.dynamic_slice_in_dim(chip_total[1], core * half, half, 2))
    row_before, row_total = ring_scan(chip_half, "ctx", count, 2, 4)
    rows = count // 8
    top_before, top_total = ring_scan(row_total, "ctx", count, 8, rows)
    chip_before = chain(top_before, row_before)
    mine = (chip_before[1], top_total[1])
    theirs = group_shift(mine, "ctx", count, 1, 2, 1)
    joined = jax.tree.map(
        lambda a, b: jnp.where(core == 0, jnp.concatenate([a, b], 2), jnp.concatenate([b, a], 2)),
        mine,
        theirs,
    )
    chip_state, final_state = joined
    s_before = jnp.where(
        core == 0, chip_state, first[0][..., None, None] * chip_state + first[1]
    )

    tails, s_before = lax.optimization_barrier((tails, s_before))
    sent = lax.ppermute(tails, "ctx", [(count - 1, count - 2)])
    tails = pick(here == count - 2, sent, tails)
    for shift in range(1, 4):
        sent = lax.ppermute(
            tails, "ctx", [(count - 2 + c, count - 2 + c - 2 * shift) for c in range(2)]
        )
        tails = pick((here >= count - 8) & ((here % 8) // 2 == 3 - shift), sent, tails)
    rows = count // 8
    for shift in range(1, rows):
        sent = lax.ppermute(
            tails, "ctx", [(count - 8 + j, count - 8 + j - 8 * shift) for j in range(8)]
        )
        tails = pick(here // 8 == rows - 1 - shift, sent, tails)

    scores = jnp.einsum("ipn,jpn->pij", c_rows, b_rows, preferred_element_type=jnp.float32)
    position = lax.iota(jnp.int32, block_len)
    causal = position[:, None] >= position[None, :]
    gaps = jnp.where(causal, cum_heads[..., :, None] - cum_heads[..., None, :], -jnp.inf)
    mixing = (scores[:, None] * jnp.exp(gaps) * dt_heads[..., None, :]).astype(jnp.bfloat16)
    y_intra = jnp.einsum("phij,jphd->iphd", mixing, x_heads, preferred_element_type=jnp.float32)
    y_inter = (
        jnp.einsum(
            "ipn,phdn->iphd", c_rows.astype(jnp.float32), s_before, precision=lax.Precision.HIGHEST
        )
        * jnp.exp(cum_log)[..., None]
    )
    y_all = y_intra + y_inter + skip[:, None] * x_heads.astype(jnp.float32)
    gated_out = y_all.reshape(block_len, prompts, inner_loc) * jax.nn.silu(z_in.astype(jnp.float32))
    square_local = jnp.sum(gated_out * gated_out, axis=-1)
    head_count = lax.axis_size("head")
    square_sums = square_local
    for shift in range(1, head_count):
        square_sums = square_sums + group_shift(square_local, "head", head_count, 1, head_count, shift)
    inner_total = inner_loc * lax.axis_size("head")
    normed = (
        gated_out * lax.rsqrt(square_sums / inner_total + norm_eps)[..., None] * norm_gain
    ).astype(jnp.bfloat16)
    projected = jnp.einsum("tpi,id->tpd", normed, w_out, preferred_element_type=jnp.float32)
    out = ring_reduce_scatter(projected, "head").astype(jnp.bfloat16)

    final_x, final_bc = tails
    slot_count = requests.shape[0]
    steps = step_x.shape[0]
    slot_pick = (requests[:, None] == lax.iota(jnp.int32, prompts)[None, :]).astype(jnp.float32)
    live_slots = requests < prompts
    hist_x = jnp.einsum(
        "rp,kpi->kri", slot_pick, final_x.astype(jnp.float32), precision=lax.Precision.HIGHEST
    ).astype(jnp.bfloat16)
    hist_bc = jnp.einsum(
        "rp,kpi->kri", slot_pick, final_bc.astype(jnp.float32), precision=lax.Precision.HIGHEST
    ).astype(jnp.bfloat16)
    window_x = jnp.concatenate([hist_x, step_x], axis=0)
    window_bc = jnp.concatenate([hist_bc, step_bc], axis=0)
    new_x = conv_silu(window_x, conv_x, steps)
    new_bc = conv_silu(window_bc, conv_bc, steps)
    dt_step = jax.nn.softplus(step_dt + dt_bias)
    x_step = new_x.reshape(steps, slot_count, heads_loc, head_dim).astype(jnp.float32)
    b_step = new_bc[..., :state_dim].astype(jnp.float32)
    c_step = new_bc[..., state_dim:].astype(jnp.float32)
    step_decay = jnp.exp(dt_step * decay_rates)
    pushed = dt_step[..., None] * x_step
    from_final = jnp.einsum(
        "phdn,srn->psrhd", final_state.reshape(prompts, heads_loc, head_dim, state_dim), c_step,
        precision=lax.Precision.HIGHEST,
    )
    from_final = jnp.einsum("rp,psrhd->srhd", slot_pick, from_final, precision=lax.Precision.HIGHEST)
    overlap = jnp.einsum("trn,srn->tsr", b_step, c_step, precision=lax.Precision.HIGHEST)
    outputs = []
    carried = jnp.ones_like(step_decay[0])
    for step_index in range(steps):
        carried = carried * step_decay[step_index]
        y_step = carried[..., None] * from_final[step_index]
        for earlier in range(step_index + 1):
            weight = jnp.ones_like(step_decay[0])
            for later in range(earlier + 1, step_index + 1):
                weight = weight * step_decay[later]
            y_step = y_step + (weight * overlap[earlier, step_index][:, None])[..., None] * pushed[
                earlier
            ]
        y_step = y_step + skip[:, None] * x_step[step_index]
        gated_step = y_step.reshape(slot_count, inner_loc) * jax.nn.silu(
            step_z[step_index].astype(jnp.float32)
        )
        outputs.append(jnp.where(live_slots[:, None], gated_step, 0.0).astype(jnp.bfloat16))
    return (out, jnp.stack(outputs))

def solution(mesh):
    placed = (
        P("ctx", None, "head"),
        P("ctx", None, "head"),
        P("ctx", None, None),
        P("ctx", None, "head"),
        P("head"),
        P("head"),
        P("head"),
        P(None, "head"),
        P(),
        P("head"),
        P("head", None),
        P("ctx"),
        P(None, "ctx", "head"),
        P(None, "ctx", "head"),
        P(None, "ctx", None),
        P(None, "ctx", "head"),
    )
    return jax.shard_map(
        body,
        mesh=mesh,
        in_specs=placed,
        out_specs=(P(("ctx", "head"), None, None), P(None, "ctx", "head")),
        check_vma=False,
    )
```

```python
import jax
import jax.numpy as jnp
from jax import lax
from jax.sharding import PartitionSpec as P

norm_eps = 1e-05


def passed_along(value, axis, steps):
    count = lax.axis_size(axis)
    leading, last = (max(0, -steps), min(count, count - steps))
    return lax.ppermute(value, axis, [(source, source + steps) for source in range(leading, last)])


def group_shift(value, axis, count, stride, group, shift):
    pairs = []
    for source in range(count):
        member = (source // stride) % group
        target = source + (((member + shift) % group) - member) * stride
        pairs.append((source, target))
    return lax.ppermute(value, axis, pairs)


def conv_silu(window, weight, length):
    running_sum = jnp.zeros((length,) + window.shape[1:], jnp.float32)
    for offset in range(weight.shape[0]):
        running_sum = running_sum + window[offset : offset + length].astype(jnp.float32) * weight[
            offset
        ].astype(jnp.float32)
    return jax.nn.silu(running_sum).astype(jnp.bfloat16)


def chain(earlier, later):
    return (earlier[0] * later[0], later[0][..., None, None] * earlier[1] + later[1])


def pick(flag, first, second):
    return jax.tree.map(lambda a, b: jnp.where(flag, a, b), first, second)


def ring_scan(own, axis, count, stride, group):
    member = (lax.axis_index(axis) // stride) % group
    if group == 4:
        from_prev = group_shift(own, axis, count, stride, group, 1)
        from_next = group_shift(own, axis, count, stride, group, -1)
        split = own[1].shape[2] // 2
        lead = group_shift(
            (from_prev[0], from_prev[1][:, :, :split]), axis, count, stride, group, 1
        )
        rest = group_shift(from_next[1][:, :, split:], axis, count, stride, group, -1)
        far = (lead[0], jnp.concatenate([lead[1], rest], 2))
        received = [None, from_prev, far, from_next]
    else:
        received = [None] + [
            group_shift(own, axis, count, stride, group, shift) for shift in range(1, group)
        ]
    identity = (jnp.ones_like(own[0]), jnp.zeros_like(own[1]))
    before = identity
    for shift in range(group - 1, 0, -1):
        before = pick(shift <= member, chain(before, received[shift]), before)
    total = chain(before, own)
    for shift in range(group - 1, 0, -1):
        total = pick(shift > member, chain(total, received[shift]), total)
    return before, total


def body(
    x_in,
    z_in,
    bc_in,
    dt_in,
    dt_bias,
    a_log,
    skip,
    conv_x,
    conv_bc,
    norm_gain,
    w_out,
    requests,
    step_x,
    step_z,
    step_bc,
    step_dt,
):
    block_len, prompts, inner_loc = x_in.shape
    heads_loc = dt_in.shape[2]
    head_dim = inner_loc // heads_loc
    state_dim = bc_in.shape[2] // 2
    conv_taps = conv_x.shape[0]
    edge_x, edge_bc = passed_along(
        (x_in[block_len - conv_taps + 1 :], bc_in[block_len - conv_taps + 1 :]), "ctx", 1
    )
    x_conv = conv_silu(jnp.concatenate([edge_x, x_in], axis=0), conv_x, block_len)
    bc_conv = conv_silu(jnp.concatenate([edge_bc, bc_in], axis=0), conv_bc, block_len)
    b_rows = bc_conv[..., :state_dim]
    c_rows = bc_conv[..., state_dim:]
    decay_rates = -jnp.exp(a_log)
    dt_full = jax.nn.softplus(dt_in + dt_bias)
    cum_log = jnp.cumsum(dt_full * decay_rates, axis=0)
    cum_heads = jnp.transpose(cum_log, (1, 2, 0))
    dt_heads = jnp.transpose(dt_full, (1, 2, 0))
    x_heads = x_conv.reshape(block_len, prompts, heads_loc, head_dim)
    block_log = cum_heads[..., -1]
    tail_weights = jnp.transpose(jnp.exp(block_log[..., None] - cum_heads) * dt_heads, (2, 0, 1))
    weighted_x = (x_heads * tail_weights[..., None]).astype(jnp.bfloat16)
    s_local = jnp.einsum("jphd,jpn->phdn", weighted_x, b_rows, preferred_element_type=jnp.float32)
    block_decay = jnp.exp(block_log)

    count = lax.axis_size("ctx")
    here = lax.axis_index("ctx")
    core = here % 2
    tails = (x_in[block_len - conv_taps + 1 :], bc_in[block_len - conv_taps + 1 :])
    reach = count // 2
    while reach >= 1:
        sent = lax.ppermute(
            tails,
            "ctx",
            [(source, source - reach) for source in range(count) if source % (2 * reach) == 2 * reach - 1],
        )
        taking = here % (2 * reach) == reach - 1
        tails = pick(taking, sent, tails)
        reach //= 2
    own = (block_decay, s_local)
    scores = jnp.einsum("ipn,jpn->pij", c_rows, b_rows, preferred_element_type=jnp.float32)
    position = lax.iota(jnp.int32, block_len)
    causal = position[:, None] >= position[None, :]
    gaps = jnp.where(causal, cum_heads[..., :, None] - cum_heads[..., None, :], -jnp.inf)
    mixing = (scores[:, None] * jnp.exp(gaps) * dt_heads[..., None, :]).astype(jnp.bfloat16)
    y_intra = jnp.einsum("phij,jphd->iphd", mixing, x_heads, preferred_element_type=jnp.float32)
    y_local = y_intra + skip[:, None] * x_heads.astype(jnp.float32)
    other = group_shift(own, "ctx", count, 1, 2, 1)
    other, y_local = lax.optimization_barrier((other, y_local))
    first = pick(core == 0, own, other)
    second = pick(core == 0, other, own)
    chip_total = chain(first, second)
    half = head_dim // 2
    chip_half = (chip_total[0], lax.dynamic_slice_in_dim(chip_total[1], core * half, half, 2))
    row_before, row_total = ring_scan(chip_half, "ctx", count, 2, 4)
    rows = count // 8
    top_before, top_total = ring_scan(row_total, "ctx", count, 8, rows)
    chip_before = chain(top_before, row_before)
    mine = (chip_before[1], top_total[1])
    theirs = group_shift(mine, "ctx", count, 1, 2, 1)
    joined = jax.tree.map(
        lambda a, b: jnp.where(core == 0, jnp.concatenate([a, b], 2), jnp.concatenate([b, a], 2)),
        mine,
        theirs,
    )
    chip_state, final_state = joined
    s_before = jnp.where(
        core == 0, chip_state, first[0][..., None, None] * chip_state + first[1]
    )

    y_inter = (
        jnp.einsum(
            "ipn,phdn->iphd", c_rows.astype(jnp.float32), s_before, precision=lax.Precision.HIGHEST
        )
        * jnp.exp(cum_log)[..., None]
    )
    y_all = y_local + y_inter
    gated_out = y_all.reshape(block_len, prompts, inner_loc) * jax.nn.silu(z_in.astype(jnp.float32))
    square_local = jnp.sum(gated_out * gated_out, axis=-1)
    head_count = lax.axis_size("head")
    square_sums = square_local
    for shift in range(1, head_count):
        square_sums = square_sums + group_shift(square_local, "head", head_count, 1, head_count, shift)
    inner_total = inner_loc * lax.axis_size("head")
    normed = (
        gated_out * lax.rsqrt(square_sums / inner_total + norm_eps)[..., None] * norm_gain
    ).astype(jnp.bfloat16)
    projected = lax.psum_scatter(
        jnp.einsum("tpi,id->tpd", normed, w_out, preferred_element_type=jnp.float32).astype(
            jnp.bfloat16
        ),
        "head",
        scatter_dimension=0,
        tiled=True,
    )
    out = projected.astype(jnp.bfloat16)

    final_x, final_bc = tails
    slot_count = requests.shape[0]
    steps = step_x.shape[0]
    slot_pick = (requests[:, None] == lax.iota(jnp.int32, prompts)[None, :]).astype(jnp.float32)
    live_slots = requests < prompts
    hist_x = jnp.einsum(
        "rp,kpi->kri", slot_pick, final_x.astype(jnp.float32), precision=lax.Precision.HIGHEST
    ).astype(jnp.bfloat16)
    hist_bc = jnp.einsum(
        "rp,kpi->kri", slot_pick, final_bc.astype(jnp.float32), precision=lax.Precision.HIGHEST
    ).astype(jnp.bfloat16)
    window_x = jnp.concatenate([hist_x, step_x], axis=0)
    window_bc = jnp.concatenate([hist_bc, step_bc], axis=0)
    new_x = conv_silu(window_x, conv_x, steps)
    new_bc = conv_silu(window_bc, conv_bc, steps)
    dt_step = jax.nn.softplus(step_dt + dt_bias)
    x_step = new_x.reshape(steps, slot_count, heads_loc, head_dim).astype(jnp.float32)
    b_step = new_bc[..., :state_dim].astype(jnp.float32)
    c_step = new_bc[..., state_dim:].astype(jnp.float32)
    step_decay = jnp.exp(dt_step * decay_rates)
    pushed = dt_step[..., None] * x_step
    from_final = jnp.einsum(
        "phdn,srn->psrhd", final_state.reshape(prompts, heads_loc, head_dim, state_dim), c_step,
        precision=lax.Precision.HIGHEST,
    )
    from_final = jnp.einsum("rp,psrhd->srhd", slot_pick, from_final, precision=lax.Precision.HIGHEST)
    overlap = jnp.einsum("trn,srn->tsr", b_step, c_step, precision=lax.Precision.HIGHEST)
    outputs = []
    carried = jnp.ones_like(step_decay[0])
    for step_index in range(steps):
        carried = carried * step_decay[step_index]
        y_step = carried[..., None] * from_final[step_index]
        for earlier in range(step_index + 1):
            weight = jnp.ones_like(step_decay[0])
            for later in range(earlier + 1, step_index + 1):
                weight = weight * step_decay[later]
            y_step = y_step + (weight * overlap[earlier, step_index][:, None])[..., None] * pushed[
                earlier
            ]
        y_step = y_step + skip[:, None] * x_step[step_index]
        gated_step = y_step.reshape(slot_count, inner_loc) * jax.nn.silu(
            step_z[step_index].astype(jnp.float32)
        )
        outputs.append(jnp.where(live_slots[:, None], gated_step, 0.0).astype(jnp.bfloat16))
    return (out, jnp.stack(outputs))

def solution(mesh):
    placed = (
        P("ctx", None, "head"),
        P("ctx", None, "head"),
        P("ctx", None, None),
        P("ctx", None, "head"),
        P("head"),
        P("head"),
        P("head"),
        P(None, "head"),
        P(),
        P("head"),
        P("head", None),
        P("ctx"),
        P(None, "ctx", "head"),
        P(None, "ctx", "head"),
        P(None, "ctx", None),
        P(None, "ctx", "head"),
    )
    return jax.shard_map(
        body,
        mesh=mesh,
        in_specs=placed,
        out_specs=(P(("ctx", "head"), None, None), P(None, "ctx", "head")),
        check_vma=False,
    )
```

```python
import jax
import jax.numpy as jnp
from jax import lax
from jax.sharding import PartitionSpec as P

norm_eps = 1e-05


def passed_along(value, axis, steps):
    count = lax.axis_size(axis)
    leading, last = (max(0, -steps), min(count, count - steps))
    return lax.ppermute(value, axis, [(source, source + steps) for source in range(leading, last)])


def group_shift(value, axis, count, stride, group, shift):
    pairs = []
    for source in range(count):
        member = (source // stride) % group
        target = source + (((member + shift) % group) - member) * stride
        pairs.append((source, target))
    return lax.ppermute(value, axis, pairs)


def conv_silu(window, weight, length):
    running_sum = jnp.zeros((length,) + window.shape[1:], jnp.float32)
    for offset in range(weight.shape[0]):
        running_sum = running_sum + window[offset : offset + length].astype(jnp.float32) * weight[
            offset
        ].astype(jnp.float32)
    return jax.nn.silu(running_sum).astype(jnp.bfloat16)


def chain(earlier, later):
    return (earlier[0] * later[0], later[0][..., None, None] * earlier[1] + later[1])


def pick(flag, first, second):
    return jax.tree.map(lambda a, b: jnp.where(flag, a, b), first, second)


def ring_scan(own, axis, count, stride, group):
    member = (lax.axis_index(axis) // stride) % group
    if group == 4:
        from_prev = group_shift(own, axis, count, stride, group, 1)
        from_next = group_shift(own, axis, count, stride, group, -1)
        split = own[1].shape[2] // 2
        lead = group_shift(
            (from_prev[0], from_prev[1][:, :, :split]), axis, count, stride, group, 1
        )
        rest = group_shift(from_next[1][:, :, split:], axis, count, stride, group, -1)
        far = (lead[0], jnp.concatenate([lead[1], rest], 2))
        received = [None, from_prev, far, from_next]
    else:
        received = [None] + [
            group_shift(own, axis, count, stride, group, shift) for shift in range(1, group)
        ]
    identity = (jnp.ones_like(own[0]), jnp.zeros_like(own[1]))
    before = identity
    for shift in range(group - 1, 0, -1):
        before = pick(shift <= member, chain(before, received[shift]), before)
    total = chain(before, own)
    for shift in range(group - 1, 0, -1):
        total = pick(shift > member, chain(total, received[shift]), total)
    return before, total


def body(
    x_in,
    z_in,
    bc_in,
    dt_in,
    dt_bias,
    a_log,
    skip,
    conv_x,
    conv_bc,
    norm_gain,
    w_out,
    requests,
    step_x,
    step_z,
    step_bc,
    step_dt,
):
    block_len, prompts, inner_loc = x_in.shape
    heads_loc = dt_in.shape[2]
    head_dim = inner_loc // heads_loc
    state_dim = bc_in.shape[2] // 2
    conv_taps = conv_x.shape[0]
    edge_x, edge_bc = passed_along(
        (x_in[block_len - conv_taps + 1 :], bc_in[block_len - conv_taps + 1 :]), "ctx", 1
    )
    x_conv = conv_silu(jnp.concatenate([edge_x, x_in], axis=0), conv_x, block_len)
    bc_conv = conv_silu(jnp.concatenate([edge_bc, bc_in], axis=0), conv_bc, block_len)
    b_rows = bc_conv[..., :state_dim]
    c_rows = bc_conv[..., state_dim:]
    decay_rates = -jnp.exp(a_log)
    dt_full = jax.nn.softplus(dt_in + dt_bias)
    cum_log = jnp.cumsum(dt_full * decay_rates, axis=0)
    cum_heads = jnp.transpose(cum_log, (1, 2, 0))
    dt_heads = jnp.transpose(dt_full, (1, 2, 0))
    x_heads = x_conv.reshape(block_len, prompts, heads_loc, head_dim)
    block_log = cum_heads[..., -1]
    tail_weights = jnp.transpose(jnp.exp(block_log[..., None] - cum_heads) * dt_heads, (2, 0, 1))
    weighted_x = (x_heads * tail_weights[..., None]).astype(jnp.bfloat16)
    s_local = jnp.einsum("jphd,jpn->phdn", weighted_x, b_rows, preferred_element_type=jnp.float32)
    block_decay = jnp.exp(block_log)

    count = lax.axis_size("ctx")
    here = lax.axis_index("ctx")
    core = here % 2
    tails = jax.tree.map(
        lambda part: lax.all_gather(part, "ctx")[count - 1],
        (x_in[block_len - conv_taps + 1 :], bc_in[block_len - conv_taps + 1 :]),
    )
    half = head_dim // 2
    keep = lax.dynamic_slice_in_dim(s_local, core * half, half, 2)
    give = lax.dynamic_slice_in_dim(s_local, (1 - core) * half, half, 2)
    other_decay, other_half = group_shift((block_decay, give), "ctx", count, 1, 2, 1)
    first_decay = jnp.where(core == 0, block_decay, other_decay)
    second_decay = jnp.where(core == 0, other_decay, block_decay)
    first_half = jnp.where(core == 0, keep, other_half)
    second_half = jnp.where(core == 0, other_half, keep)
    chip_half = (
        first_decay * second_decay,
        second_decay[..., None, None] * first_half + second_half,
    )
    row_before, row_total = ring_scan(chip_half, "ctx", count, 2, 4)
    rows = count // 8
    top_before, top_total = ring_scan(row_total, "ctx", count, 8, rows)
    chip_before = chain(top_before, row_before)
    finished = jnp.where(
        core == 0, chip_before[1], first_decay[..., None, None] * chip_before[1] + first_half
    )
    sent = jnp.where(
        core == 0, first_decay[..., None, None] * chip_before[1] + keep, chip_before[1]
    )
    theirs = group_shift((sent, top_total[1]), "ctx", count, 1, 2, 1)
    s_before = jnp.where(
        core == 0,
        jnp.concatenate([finished, theirs[0]], 2),
        jnp.concatenate([theirs[0], finished], 2),
    )
    final_state = jnp.where(
        core == 0,
        jnp.concatenate([top_total[1], theirs[1]], 2),
        jnp.concatenate([theirs[1], top_total[1]], 2),
    )

    scores = jnp.einsum("ipn,jpn->pij", c_rows, b_rows, preferred_element_type=jnp.float32)
    position = lax.iota(jnp.int32, block_len)
    causal = position[:, None] >= position[None, :]
    gaps = jnp.where(causal, cum_heads[..., :, None] - cum_heads[..., None, :], -jnp.inf)
    mixing = (scores[:, None] * jnp.exp(gaps) * dt_heads[..., None, :]).astype(jnp.bfloat16)
    y_intra = jnp.einsum("phij,jphd->iphd", mixing, x_heads, preferred_element_type=jnp.float32)
    y_inter = (
        jnp.einsum(
            "ipn,phdn->iphd", c_rows.astype(jnp.float32), s_before, precision=lax.Precision.HIGHEST
        )
        * jnp.exp(cum_log)[..., None]
    )
    y_all = y_intra + y_inter + skip[:, None] * x_heads.astype(jnp.float32)
    gated_out = y_all.reshape(block_len, prompts, inner_loc) * jax.nn.silu(z_in.astype(jnp.float32))
    square_local = jnp.sum(gated_out * gated_out, axis=-1)
    head_count = lax.axis_size("head")
    square_sums = square_local
    for shift in range(1, head_count):
        square_sums = square_sums + group_shift(square_local, "head", head_count, 1, head_count, shift)
    inner_total = inner_loc * lax.axis_size("head")
    normed = (
        gated_out * lax.rsqrt(square_sums / inner_total + norm_eps)[..., None] * norm_gain
    ).astype(jnp.bfloat16)
    projected = lax.psum_scatter(
        jnp.einsum("tpi,id->tpd", normed, w_out, preferred_element_type=jnp.float32).astype(
            jnp.bfloat16
        ),
        "head",
        scatter_dimension=0,
        tiled=True,
    )
    out = projected.astype(jnp.bfloat16)

    final_x, final_bc = tails
    slot_count = requests.shape[0]
    steps = step_x.shape[0]
    slot_pick = (requests[:, None] == lax.iota(jnp.int32, prompts)[None, :]).astype(jnp.float32)
    live_slots = requests < prompts
    hist_x = jnp.einsum(
        "rp,kpi->kri", slot_pick, final_x.astype(jnp.float32), precision=lax.Precision.HIGHEST
    ).astype(jnp.bfloat16)
    hist_bc = jnp.einsum(
        "rp,kpi->kri", slot_pick, final_bc.astype(jnp.float32), precision=lax.Precision.HIGHEST
    ).astype(jnp.bfloat16)
    window_x = jnp.concatenate([hist_x, step_x], axis=0)
    window_bc = jnp.concatenate([hist_bc, step_bc], axis=0)
    new_x = conv_silu(window_x, conv_x, steps)
    new_bc = conv_silu(window_bc, conv_bc, steps)
    dt_step = jax.nn.softplus(step_dt + dt_bias)
    x_step = new_x.reshape(steps, slot_count, heads_loc, head_dim).astype(jnp.float32)
    b_step = new_bc[..., :state_dim].astype(jnp.float32)
    c_step = new_bc[..., state_dim:].astype(jnp.float32)
    step_decay = jnp.exp(dt_step * decay_rates)
    pushed = dt_step[..., None] * x_step
    from_final = jnp.einsum(
        "phdn,srn->psrhd", final_state.reshape(prompts, heads_loc, head_dim, state_dim), c_step,
        precision=lax.Precision.HIGHEST,
    )
    from_final = jnp.einsum("rp,psrhd->srhd", slot_pick, from_final, precision=lax.Precision.HIGHEST)
    overlap = jnp.einsum("trn,srn->tsr", b_step, c_step, precision=lax.Precision.HIGHEST)
    outputs = []
    carried = jnp.ones_like(step_decay[0])
    for step_index in range(steps):
        carried = carried * step_decay[step_index]
        y_step = carried[..., None] * from_final[step_index]
        for earlier in range(step_index + 1):
            weight = jnp.ones_like(step_decay[0])
            for later in range(earlier + 1, step_index + 1):
                weight = weight * step_decay[later]
            y_step = y_step + (weight * overlap[earlier, step_index][:, None])[..., None] * pushed[
                earlier
            ]
        y_step = y_step + skip[:, None] * x_step[step_index]
        gated_step = y_step.reshape(slot_count, inner_loc) * jax.nn.silu(
            step_z[step_index].astype(jnp.float32)
        )
        outputs.append(jnp.where(live_slots[:, None], gated_step, 0.0).astype(jnp.bfloat16))
    return (out, jnp.stack(outputs))

def solution(mesh):
    placed = (
        P("ctx", None, "head"),
        P("ctx", None, "head"),
        P("ctx", None, None),
        P("ctx", None, "head"),
        P("head"),
        P("head"),
        P("head"),
        P(None, "head"),
        P(),
        P("head"),
        P("head", None),
        P("ctx"),
        P(None, "ctx", "head"),
        P(None, "ctx", "head"),
        P(None, "ctx", None),
        P(None, "ctx", "head"),
    )
    return jax.shard_map(
        body,
        mesh=mesh,
        in_specs=placed,
        out_specs=(P(("ctx", "head"), None, None), P(None, "ctx", "head")),
        check_vma=False,
    )
```

```python
import jax
import jax.numpy as jnp
from jax import lax
from jax.sharding import PartitionSpec as P

norm_eps = 1e-05


def passed_along(value, axis, steps):
    count = lax.axis_size(axis)
    leading, last = (max(0, -steps), min(count, count - steps))
    return lax.ppermute(value, axis, [(source, source + steps) for source in range(leading, last)])


def group_shift(value, axis, count, stride, group, shift):
    pairs = []
    for source in range(count):
        member = (source // stride) % group
        target = source + (((member + shift) % group) - member) * stride
        pairs.append((source, target))
    return lax.ppermute(value, axis, pairs)


def conv_silu(window, weight, length):
    running_sum = jnp.zeros((length,) + window.shape[1:], jnp.float32)
    for offset in range(weight.shape[0]):
        running_sum = running_sum + window[offset : offset + length].astype(jnp.float32) * weight[
            offset
        ].astype(jnp.float32)
    return jax.nn.silu(running_sum).astype(jnp.bfloat16)


def chain(earlier, later):
    return (earlier[0] * later[0], later[0][..., None, None] * earlier[1] + later[1])


def pick(flag, first, second):
    return jax.tree.map(lambda a, b: jnp.where(flag, a, b), first, second)


def ring_scan(own, axis, count, stride, group):
    member = (lax.axis_index(axis) // stride) % group
    if group == 4:
        from_prev = group_shift(own, axis, count, stride, group, 1)
        from_next = group_shift(own, axis, count, stride, group, -1)
        split = own[1].shape[2] // 2
        lead = group_shift(
            (from_prev[0], from_prev[1][:, :, :split]), axis, count, stride, group, 1
        )
        rest = group_shift(from_next[1][:, :, split:], axis, count, stride, group, -1)
        far = (lead[0], jnp.concatenate([lead[1], rest], 2))
        received = [None, from_prev, far, from_next]
    else:
        received = [None] + [
            group_shift(own, axis, count, stride, group, shift) for shift in range(1, group)
        ]
    identity = (jnp.ones_like(own[0]), jnp.zeros_like(own[1]))
    before = identity
    for shift in range(group - 1, 0, -1):
        before = pick(shift <= member, chain(before, received[shift]), before)
    total = chain(before, own)
    for shift in range(group - 1, 0, -1):
        total = pick(shift > member, chain(total, received[shift]), total)
    return before, total


def body(
    x_in,
    z_in,
    bc_in,
    dt_in,
    dt_bias,
    a_log,
    skip,
    conv_x,
    conv_bc,
    norm_gain,
    w_out,
    requests,
    step_x,
    step_z,
    step_bc,
    step_dt,
):
    block_len, prompts, inner_loc = x_in.shape
    heads_loc = dt_in.shape[2]
    head_dim = inner_loc // heads_loc
    state_dim = bc_in.shape[2] // 2
    conv_taps = conv_x.shape[0]
    edge_x, edge_bc = passed_along(
        (x_in[block_len - conv_taps + 1 :], bc_in[block_len - conv_taps + 1 :]), "ctx", 1
    )
    x_conv = conv_silu(jnp.concatenate([edge_x, x_in], axis=0), conv_x, block_len)
    bc_conv = conv_silu(jnp.concatenate([edge_bc, bc_in], axis=0), conv_bc, block_len)
    b_rows = bc_conv[..., :state_dim]
    c_rows = bc_conv[..., state_dim:]
    decay_rates = -jnp.exp(a_log)
    dt_full = jax.nn.softplus(dt_in + dt_bias)
    cum_log = jnp.cumsum(dt_full * decay_rates, axis=0)
    cum_heads = jnp.transpose(cum_log, (1, 2, 0))
    dt_heads = jnp.transpose(dt_full, (1, 2, 0))
    x_heads = x_conv.reshape(block_len, prompts, heads_loc, head_dim)
    block_log = cum_heads[..., -1]
    tail_weights = jnp.transpose(jnp.exp(block_log[..., None] - cum_heads) * dt_heads, (2, 0, 1))
    weighted_x = (x_heads * tail_weights[..., None]).astype(jnp.bfloat16)
    s_local = jnp.einsum("jphd,jpn->phdn", weighted_x, b_rows, preferred_element_type=jnp.float32)
    block_decay = jnp.exp(block_log)

    count = lax.axis_size("ctx")
    here = lax.axis_index("ctx")
    core = here % 2
    history = lax.all_gather(
        jnp.concatenate([x_in[block_len - conv_taps + 1 :], bc_in[block_len - conv_taps + 1 :]], -1),
        "ctx",
    )[count - 1]
    tails = (history[..., :inner_loc], history[..., inner_loc:])
    half = head_dim // 2
    keep = lax.dynamic_slice_in_dim(s_local, core * half, half, 2)
    give = lax.dynamic_slice_in_dim(s_local, (1 - core) * half, half, 2)
    other_decay, other_half = group_shift((block_decay, give), "ctx", count, 1, 2, 1)
    first_decay = jnp.where(core == 0, block_decay, other_decay)
    second_decay = jnp.where(core == 0, other_decay, block_decay)
    first_half = jnp.where(core == 0, keep, other_half)
    second_half = jnp.where(core == 0, other_half, keep)
    chip_half = (
        first_decay * second_decay,
        second_decay[..., None, None] * first_half + second_half,
    )
    row_before, row_total = ring_scan(chip_half, "ctx", count, 2, 4)
    rows = count // 8
    top_before, top_total = ring_scan(row_total, "ctx", count, 8, rows)
    chip_before = chain(top_before, row_before)
    finished = jnp.where(
        core == 0, chip_before[1], first_decay[..., None, None] * chip_before[1] + first_half
    )
    sent = jnp.where(
        core == 0, first_decay[..., None, None] * chip_before[1] + keep, chip_before[1]
    )
    theirs = group_shift((sent, top_total[1]), "ctx", count, 1, 2, 1)
    s_before = jnp.where(
        core == 0,
        jnp.concatenate([finished, theirs[0]], 2),
        jnp.concatenate([theirs[0], finished], 2),
    )
    final_state = jnp.where(
        core == 0,
        jnp.concatenate([top_total[1], theirs[1]], 2),
        jnp.concatenate([theirs[1], top_total[1]], 2),
    )

    scores = jnp.einsum("ipn,jpn->pij", c_rows, b_rows, preferred_element_type=jnp.float32)
    position = lax.iota(jnp.int32, block_len)
    causal = position[:, None] >= position[None, :]
    gaps = jnp.where(causal, cum_heads[..., :, None] - cum_heads[..., None, :], -jnp.inf)
    mixing = (scores[:, None] * jnp.exp(gaps) * dt_heads[..., None, :]).astype(jnp.bfloat16)
    y_intra = jnp.einsum("phij,jphd->iphd", mixing, x_heads, preferred_element_type=jnp.float32)
    y_inter = (
        jnp.einsum(
            "ipn,phdn->iphd", c_rows.astype(jnp.float32), s_before, precision=lax.Precision.HIGHEST
        )
        * jnp.exp(cum_log)[..., None]
    )
    y_all = y_intra + y_inter + skip[:, None] * x_heads.astype(jnp.float32)
    gated_out = y_all.reshape(block_len, prompts, inner_loc) * jax.nn.silu(z_in.astype(jnp.float32))
    square_local = jnp.sum(gated_out * gated_out, axis=-1)
    head_count = lax.axis_size("head")
    square_sums = square_local
    for shift in range(1, head_count):
        square_sums = square_sums + group_shift(square_local, "head", head_count, 1, head_count, shift)
    inner_total = inner_loc * lax.axis_size("head")
    normed = (
        gated_out * lax.rsqrt(square_sums / inner_total + norm_eps)[..., None] * norm_gain
    ).astype(jnp.bfloat16)
    projected = lax.psum_scatter(
        jnp.einsum("tpi,id->tpd", normed, w_out, preferred_element_type=jnp.float32).astype(
            jnp.bfloat16
        ),
        "head",
        scatter_dimension=0,
        tiled=True,
    )
    out = projected.astype(jnp.bfloat16)

    final_x, final_bc = tails
    slot_count = requests.shape[0]
    steps = step_x.shape[0]
    slot_pick = (requests[:, None] == lax.iota(jnp.int32, prompts)[None, :]).astype(jnp.float32)
    live_slots = requests < prompts
    hist_x = jnp.einsum(
        "rp,kpi->kri", slot_pick, final_x.astype(jnp.float32), precision=lax.Precision.HIGHEST
    ).astype(jnp.bfloat16)
    hist_bc = jnp.einsum(
        "rp,kpi->kri", slot_pick, final_bc.astype(jnp.float32), precision=lax.Precision.HIGHEST
    ).astype(jnp.bfloat16)
    window_x = jnp.concatenate([hist_x, step_x], axis=0)
    window_bc = jnp.concatenate([hist_bc, step_bc], axis=0)
    new_x = conv_silu(window_x, conv_x, steps)
    new_bc = conv_silu(window_bc, conv_bc, steps)
    dt_step = jax.nn.softplus(step_dt + dt_bias)
    x_step = new_x.reshape(steps, slot_count, heads_loc, head_dim).astype(jnp.float32)
    b_step = new_bc[..., :state_dim].astype(jnp.float32)
    c_step = new_bc[..., state_dim:].astype(jnp.float32)
    step_decay = jnp.exp(dt_step * decay_rates)
    pushed = dt_step[..., None] * x_step
    from_final = jnp.einsum(
        "phdn,srn->psrhd", final_state.reshape(prompts, heads_loc, head_dim, state_dim), c_step,
        precision=lax.Precision.HIGHEST,
    )
    from_final = jnp.einsum("rp,psrhd->srhd", slot_pick, from_final, precision=lax.Precision.HIGHEST)
    overlap = jnp.einsum("trn,srn->tsr", b_step, c_step, precision=lax.Precision.HIGHEST)
    outputs = []
    carried = jnp.ones_like(step_decay[0])
    for step_index in range(steps):
        carried = carried * step_decay[step_index]
        y_step = carried[..., None] * from_final[step_index]
        for earlier in range(step_index + 1):
            weight = jnp.ones_like(step_decay[0])
            for later in range(earlier + 1, step_index + 1):
                weight = weight * step_decay[later]
            y_step = y_step + (weight * overlap[earlier, step_index][:, None])[..., None] * pushed[
                earlier
            ]
        y_step = y_step + skip[:, None] * x_step[step_index]
        gated_step = y_step.reshape(slot_count, inner_loc) * jax.nn.silu(
            step_z[step_index].astype(jnp.float32)
        )
        outputs.append(jnp.where(live_slots[:, None], gated_step, 0.0).astype(jnp.bfloat16))
    return (out, jnp.stack(outputs))

def solution(mesh):
    placed = (
        P("ctx", None, "head"),
        P("ctx", None, "head"),
        P("ctx", None, None),
        P("ctx", None, "head"),
        P("head"),
        P("head"),
        P("head"),
        P(None, "head"),
        P(),
        P("head"),
        P("head", None),
        P("ctx"),
        P(None, "ctx", "head"),
        P(None, "ctx", "head"),
        P(None, "ctx", None),
        P(None, "ctx", "head"),
    )
    return jax.shard_map(
        body,
        mesh=mesh,
        in_specs=placed,
        out_specs=(P(("ctx", "head"), None, None), P(None, "ctx", "head")),
        check_vma=False,
    )
```

```python
import jax
import jax.numpy as jnp
from jax import lax
from jax.sharding import PartitionSpec as P

norm_eps = 1e-05


def passed_along(value, axis, steps):
    count = lax.axis_size(axis)
    leading, last = (max(0, -steps), min(count, count - steps))
    return lax.ppermute(value, axis, [(source, source + steps) for source in range(leading, last)])


def group_shift(value, axis, count, stride, group, shift):
    pairs = []
    for source in range(count):
        member = (source // stride) % group
        target = source + (((member + shift) % group) - member) * stride
        pairs.append((source, target))
    return lax.ppermute(value, axis, pairs)


def conv_silu(window, weight, length):
    running_sum = jnp.zeros((length,) + window.shape[1:], jnp.float32)
    for offset in range(weight.shape[0]):
        running_sum = running_sum + window[offset : offset + length].astype(jnp.float32) * weight[
            offset
        ].astype(jnp.float32)
    return jax.nn.silu(running_sum).astype(jnp.bfloat16)


def chain(earlier, later):
    return (earlier[0] * later[0], later[0][..., None, None] * earlier[1] + later[1])


def pick(flag, first, second):
    return jax.tree.map(lambda a, b: jnp.where(flag, a, b), first, second)


def ring_scan(own, axis, count, stride, group):
    member = (lax.axis_index(axis) // stride) % group
    if group == 4:
        from_prev = group_shift(own, axis, count, stride, group, 1)
        from_next = group_shift(own, axis, count, stride, group, -1)
        split = own[1].shape[2] // 2
        lead = group_shift(
            (from_prev[0], from_prev[1][:, :, :split]), axis, count, stride, group, 1
        )
        rest = group_shift(from_next[1][:, :, split:], axis, count, stride, group, -1)
        far = (lead[0], jnp.concatenate([lead[1], rest], 2))
        received = [None, from_prev, far, from_next]
    else:
        received = [None] + [
            group_shift(own, axis, count, stride, group, shift) for shift in range(1, group)
        ]
    identity = (jnp.ones_like(own[0]), jnp.zeros_like(own[1]))
    before = identity
    for shift in range(group - 1, 0, -1):
        before = pick(shift <= member, chain(before, received[shift]), before)
    total = chain(before, own)
    for shift in range(group - 1, 0, -1):
        total = pick(shift > member, chain(total, received[shift]), total)
    return before, total


def body(
    x_in,
    z_in,
    bc_in,
    dt_in,
    dt_bias,
    a_log,
    skip,
    conv_x,
    conv_bc,
    norm_gain,
    w_out,
    requests,
    step_x,
    step_z,
    step_bc,
    step_dt,
):
    block_len, prompts, inner_loc = x_in.shape
    heads_loc = dt_in.shape[2]
    head_dim = inner_loc // heads_loc
    state_dim = bc_in.shape[2] // 2
    conv_taps = conv_x.shape[0]
    edge_x, edge_bc = passed_along(
        (x_in[block_len - conv_taps + 1 :], bc_in[block_len - conv_taps + 1 :]), "ctx", 1
    )
    x_conv = conv_silu(jnp.concatenate([edge_x, x_in], axis=0), conv_x, block_len)
    bc_conv = conv_silu(jnp.concatenate([edge_bc, bc_in], axis=0), conv_bc, block_len)
    b_rows = bc_conv[..., :state_dim]
    c_rows = bc_conv[..., state_dim:]
    decay_rates = -jnp.exp(a_log)
    dt_full = jax.nn.softplus(dt_in + dt_bias)
    cum_log = jnp.cumsum(dt_full * decay_rates, axis=0)
    cum_heads = jnp.transpose(cum_log, (1, 2, 0))
    dt_heads = jnp.transpose(dt_full, (1, 2, 0))
    x_heads = x_conv.reshape(block_len, prompts, heads_loc, head_dim)
    block_log = cum_heads[..., -1]
    tail_weights = jnp.transpose(jnp.exp(block_log[..., None] - cum_heads) * dt_heads, (2, 0, 1))
    weighted_x = (x_heads * tail_weights[..., None]).astype(jnp.bfloat16)
    s_local = jnp.einsum("jphd,jpn->phdn", weighted_x, b_rows, preferred_element_type=jnp.float32)
    block_decay = jnp.exp(block_log)

    count = lax.axis_size("ctx")
    here = lax.axis_index("ctx")
    core = here % 2
    history = lax.all_gather(
        jnp.concatenate([x_in[block_len - conv_taps + 1 :], bc_in[block_len - conv_taps + 1 :]], -1),
        "ctx",
    )[count - 1]
    tails = (history[..., :inner_loc], history[..., inner_loc:])
    half = head_dim // 2
    keep = lax.dynamic_slice_in_dim(s_local, core * half, half, 2)
    give = lax.dynamic_slice_in_dim(s_local, (1 - core) * half, half, 2)
    other_decay, other_half = group_shift((block_decay, give), "ctx", count, 1, 2, 1)
    first_decay = jnp.where(core == 0, block_decay, other_decay)
    second_decay = jnp.where(core == 0, other_decay, block_decay)
    first_half = jnp.where(core == 0, keep, other_half)
    second_half = jnp.where(core == 0, other_half, keep)
    chip_half = (
        first_decay * second_decay,
        second_decay[..., None, None] * first_half + second_half,
    )
    row_before, row_total = ring_scan(chip_half, "ctx", count, 2, 4)
    rows = count // 8
    top_before, top_total = ring_scan(row_total, "ctx", count, 8, rows)
    chip_before = chain(top_before, row_before)
    finished = jnp.where(
        core == 0, chip_before[1], first_decay[..., None, None] * chip_before[1] + first_half
    )
    sent = jnp.where(
        core == 0, first_decay[..., None, None] * chip_before[1] + keep, chip_before[1]
    )
    theirs = group_shift((sent, top_total[1]), "ctx", count, 1, 2, 1)
    s_before = jnp.where(
        core == 0,
        jnp.concatenate([finished, theirs[0]], 2),
        jnp.concatenate([theirs[0], finished], 2),
    )
    final_state = jnp.where(
        core == 0,
        jnp.concatenate([top_total[1], theirs[1]], 2),
        jnp.concatenate([theirs[1], top_total[1]], 2),
    )

    scores = jnp.einsum("ipn,jpn->pij", c_rows, b_rows, preferred_element_type=jnp.float32)
    position = lax.iota(jnp.int32, block_len)
    causal = position[:, None] >= position[None, :]
    gaps = jnp.where(causal, cum_heads[..., :, None] - cum_heads[..., None, :], -jnp.inf)
    mixing = (scores[:, None] * jnp.exp(gaps) * dt_heads[..., None, :]).astype(jnp.bfloat16)
    y_intra = jnp.einsum("phij,jphd->iphd", mixing, x_heads, preferred_element_type=jnp.float32)
    y_inter = (
        jnp.einsum(
            "ipn,phdn->iphd", c_rows.astype(jnp.float32), s_before, precision=lax.Precision.HIGHEST
        )
        * jnp.exp(cum_log)[..., None]
    )
    y_all = y_intra + y_inter + skip[:, None] * x_heads.astype(jnp.float32)
    gated_out = y_all.reshape(block_len, prompts, inner_loc) * jax.nn.silu(z_in.astype(jnp.float32))
    square_local = jnp.sum(gated_out * gated_out, axis=-1)
    head_count = lax.axis_size("head")
    square_sums = square_local
    for shift in range(1, head_count):
        square_sums = square_sums + group_shift(square_local, "head", head_count, 1, head_count, shift)
    inner_total = inner_loc * lax.axis_size("head")
    normed = (
        gated_out * lax.rsqrt(square_sums / inner_total + norm_eps)[..., None] * norm_gain
    ).astype(jnp.bfloat16)
    normed = lax.optimization_barrier(normed)
    projected = lax.psum_scatter(
        jnp.einsum("tpi,id->tpd", normed, w_out, preferred_element_type=jnp.float32).astype(
            jnp.bfloat16
        ),
        "head",
        scatter_dimension=0,
        tiled=True,
    )
    out = projected.astype(jnp.bfloat16)

    final_x, final_bc = tails
    slot_count = requests.shape[0]
    steps = step_x.shape[0]
    slot_pick = (requests[:, None] == lax.iota(jnp.int32, prompts)[None, :]).astype(jnp.float32)
    live_slots = requests < prompts
    hist_x = jnp.einsum(
        "rp,kpi->kri", slot_pick, final_x.astype(jnp.float32), precision=lax.Precision.HIGHEST
    ).astype(jnp.bfloat16)
    hist_bc = jnp.einsum(
        "rp,kpi->kri", slot_pick, final_bc.astype(jnp.float32), precision=lax.Precision.HIGHEST
    ).astype(jnp.bfloat16)
    window_x = jnp.concatenate([hist_x, step_x], axis=0)
    window_bc = jnp.concatenate([hist_bc, step_bc], axis=0)
    new_x = conv_silu(window_x, conv_x, steps)
    new_bc = conv_silu(window_bc, conv_bc, steps)
    dt_step = jax.nn.softplus(step_dt + dt_bias)
    x_step = new_x.reshape(steps, slot_count, heads_loc, head_dim).astype(jnp.float32)
    b_step = new_bc[..., :state_dim].astype(jnp.float32)
    c_step = new_bc[..., state_dim:].astype(jnp.float32)
    step_decay = jnp.exp(dt_step * decay_rates)
    pushed = dt_step[..., None] * x_step
    from_final = jnp.einsum(
        "phdn,srn->psrhd", final_state.reshape(prompts, heads_loc, head_dim, state_dim), c_step,
        precision=lax.Precision.HIGHEST,
    )
    from_final = jnp.einsum("rp,psrhd->srhd", slot_pick, from_final, precision=lax.Precision.HIGHEST)
    overlap = jnp.einsum("trn,srn->tsr", b_step, c_step, precision=lax.Precision.HIGHEST)
    outputs = []
    carried = jnp.ones_like(step_decay[0])
    for step_index in range(steps):
        carried = carried * step_decay[step_index]
        y_step = carried[..., None] * from_final[step_index]
        for earlier in range(step_index + 1):
            weight = jnp.ones_like(step_decay[0])
            for later in range(earlier + 1, step_index + 1):
                weight = weight * step_decay[later]
            y_step = y_step + (weight * overlap[earlier, step_index][:, None])[..., None] * pushed[
                earlier
            ]
        y_step = y_step + skip[:, None] * x_step[step_index]
        gated_step = y_step.reshape(slot_count, inner_loc) * jax.nn.silu(
            step_z[step_index].astype(jnp.float32)
        )
        outputs.append(jnp.where(live_slots[:, None], gated_step, 0.0).astype(jnp.bfloat16))
    return (out, jnp.stack(outputs))

def solution(mesh):
    placed = (
        P("ctx", None, "head"),
        P("ctx", None, "head"),
        P("ctx", None, None),
        P("ctx", None, "head"),
        P("head"),
        P("head"),
        P("head"),
        P(None, "head"),
        P(),
        P("head"),
        P("head", None),
        P("ctx"),
        P(None, "ctx", "head"),
        P(None, "ctx", "head"),
        P(None, "ctx", None),
        P(None, "ctx", "head"),
    )
    return jax.shard_map(
        body,
        mesh=mesh,
        in_specs=placed,
        out_specs=(P(("ctx", "head"), None, None), P(None, "ctx", "head")),
        check_vma=False,
    )
```
